512 devices in a mesh: segment: 32 (over z, y_lo), blk: 16 (over x, y_hi, core).
Axes of the slice: x: 4, y: 8 (y_hi: 2, y_lo: 4; y = y_hi * 4 + y_lo), z: 8, core: 2. Of those that a mesh axis runs over, the one named last changes fastest.
Arguments:
- arriving: bfloat16 [32, 512, 1152], P('segment', 'blk'), may hold values from -6 to 6
- entering: bfloat16 [2, 2, 512, 1152], P(None, None, 'blk'), may hold values from -6 to 6
- section_start: int32 [16], replicated, may hold values from 0 to 27, as said below
- timestep: int32 [1], replicated, may hold values from 0 to 999
- qkv_weight: bfloat16 [32, 576, 3456], P('segment', None, 'blk'), may hold values from -0.1875 to 0.1875
- out_weight: bfloat16 [32, 576, 1152], P('segment', 'blk'), may hold values from -0.1875 to 0.1875
- stale_kv: bfloat16 [32, 1024, 2304], P('segment', None, 'blk'), may hold values from -120 to 120
- layer_table: bfloat16 [28, 3, 1152], replicated, may hold values from -3 to 3
- time_proj: bfloat16 [256, 3456], replicated, may hold values from -0.75 to 0.75
- final_table: float32 [2, 1152], replicated, may hold values from -3 to 3
- final_weight: bfloat16 [1152, 32], replicated, may hold values from -0.1875 to 0.1875
Outputs:
- waiting: bfloat16 [32, 512, 1152], P('segment', 'blk')
- noise_pred: bfloat16 [2, 2, 512, 32], P(None, None, 'blk', 'segment')
The draws below stay inside these ranges and needn't reach their ends.
Inputs may be any that keep to these rules, and one draw needn't show every extreme that they name: `section_start`: section 0 starts at layer 0; from one section to the next the start rises by 1, 2 or 3; the last section starts at layer 27.
All inputs are finite; a program needn't handle non-finite values.
Results may differ from the reference program's by a relative error of at most 0.04.
Values may be sent and summed in bfloat16 or wider, within the bound.
No kernel may reach another device: no remote copies, remote signals or barrier semaphores. Data moves between devices by JAX's collectives and lax.ppermute only.
A program may use at most 64 MiB of HBM per device.

```python
import jax
import jax.numpy as jnp
from jax import lax

D = 1152
HEADS = 16
FREQ = 256
PATCH_OUT = 32
TICKS = 2
PATCHES = 4
HEAD_DIM = 72
SEGMENTS = 16
SEQ = 512
IMAGE = 2048
TABLE_ROWS = 28


def draw_section_start(key, part):
    group_count = SEGMENTS // 4
    patterns = jnp.array([[2, 2, 2, 1], [1, 2, 3, 1], [1, 3, 2, 1], [2, 1, 3, 1], [2, 3, 1, 1], [3, 1, 2, 1], [3, 2, 1, 1]], dtype=jnp.int32)
    picked = jax.random.randint(jax.random.fold_in(key, 3), (group_count,), 0, 7)
    depths = patterns[picked].reshape(4 * group_count)
    return (jnp.cumsum(depths) - depths).astype(jnp.int32)


def draw_stale_kv(key, part):
    shape = (2 * SEGMENTS, IMAGE // 2, 2 * D)
    values = jnp.clip(1.5 * jax.random.normal(jax.random.fold_in(key, 14), shape, jnp.float32), -9.0, 9.0)
    return values.astype(jnp.bfloat16)


def shard_levels(rng, extent, pieces, least, top_value):
    loudness = 1.0
    for dim, parts in pieces:
        steps = jax.random.uniform(jax.random.fold_in(jax.random.fold_in(rng, 6), dim), (parts,), jnp.float32, least / len(pieces), top_value / len(pieces))
        loudness = loudness * jnp.repeat(jnp.exp(steps), extent[dim] // parts).reshape((-1,) + (1,) * (len(extent) - 1 - dim))
    return loudness


def normal_values(own_key, dims, width, limit, shards=(), kind=jnp.bfloat16):
    values = jax.random.normal(own_key, dims, jnp.float32) * width
    if len(shards) > 0:
        values = shard_levels(own_key, dims, shards, -0.22, 0.18) * values
    return jnp.clip(values, min=-limit, max=limit).astype(kind)


def setup_inputs(seed: int = 0) -> dict:
    streams_of = jax.random.split(jax.random.key(seed), 12)
    return {
        "arriving": normal_values(streams_of[0], (2 * SEGMENTS, SEQ, D), 1.0, 6.0, ((0, 32), (1, 16))),
        "entering": normal_values(streams_of[1], (TICKS, 2, SEQ, D), 1.0, 6.0, ((2, 16),)),
        "section_start": draw_section_start(jax.random.fold_in(streams_of[11], 71), 0),
        "timestep": jax.random.randint(streams_of[3], (1,), 0, 1000).astype(jnp.int32),
        "qkv_weight": normal_values(streams_of[4], (2 * SEGMENTS, D // 2, 3 * D), D ** -0.5, 0.1875, ((0, 32), (2, 16))),
        "out_weight": normal_values(streams_of[5], (2 * SEGMENTS, D // 2, D), D ** -0.5, 0.1875, ((0, 32), (1, 16))),
        "stale_kv": draw_stale_kv(jax.random.fold_in(streams_of[11], 71), 0),
        "layer_table": normal_values(streams_of[7], (TABLE_ROWS, 3, D), 0.5, 3.0),
        "time_proj": normal_values(streams_of[8], (FREQ, 3 * D), (FREQ // 4) ** -0.5, 0.75),
        "final_table": normal_values(streams_of[9], (2, D), 0.5, 3.0, (), jnp.float32),
        "final_weight": normal_values(streams_of[10], (D, PATCH_OUT), D ** -0.5, 0.1875),
    }


epsilon = 1e-06

def time_vector(timestep, time_proj):
    half_freq = FREQ // 2
    steps_k = jnp.arange(half_freq, dtype=jnp.float32)
    frequency = jnp.exp(-jnp.log(10000.0) * steps_k / half_freq)
    angles = timestep[0].astype(jnp.float32) * frequency
    embedding = jnp.concatenate([jnp.cos(angles), jnp.sin(angles)])
    time_feature = jax.nn.silu(embedding).astype(jnp.bfloat16)
    return jnp.dot(time_feature[None, :], time_proj, preferred_element_type=jnp.float32).reshape(3, D)

def layer_norm(values):
    widened = values.astype(jnp.float32)
    average = lax.optimization_barrier(jnp.mean(widened, axis=-1, keepdims=True))
    centred = widened - average
    variance = lax.optimization_barrier(jnp.mean(centred * centred, axis=-1, keepdims=True))
    return centred * lax.rsqrt(variance + epsilon)

def attend_head(packed):
    queries, keys_all, values_all = packed
    scores = jnp.dot(queries, keys_all.T, preferred_element_type=jnp.float32) * HEAD_DIM ** (-0.5)
    weights = jnp.exp(scores - lax.optimization_barrier(jnp.max(scores, axis=1, keepdims=True)))
    probability = (weights / lax.optimization_barrier(jnp.sum(weights, axis=1, keepdims=True))).astype(jnp.bfloat16)
    return jnp.dot(probability, values_all, preferred_element_type=jnp.float32).astype(jnp.bfloat16)

def apply_layer(holding, table_row, patch, section, qkv_sections, out_sections, stale_sections, time_mod):
    qkv_full = lax.dynamic_index_in_dim(qkv_sections, section, 0, keepdims=False)
    out_full = lax.dynamic_index_in_dim(out_sections, section, 0, keepdims=False)
    stale_full = lax.dynamic_index_in_dim(stale_sections, section, 0, keepdims=False)
    modulation = table_row.astype(jnp.float32) + time_mod
    normed = (layer_norm(holding) * (1.0 + modulation[1]) + modulation[0]).astype(jnp.bfloat16)
    projected = jnp.dot(normed, qkv_full, preferred_element_type=jnp.float32).astype(jnp.bfloat16)
    projected = projected.reshape(SEQ, HEADS, 3, HEAD_DIM)
    fresh_kv = projected[:, :, 1:3].reshape(SEQ, 2 * D)
    start_row = (patch * SEQ).astype(jnp.int32)
    kv_all = lax.dynamic_update_slice(stale_full, fresh_kv, (start_row, jnp.zeros((), jnp.int32)))
    kv_heads = kv_all.reshape(IMAGE, HEADS, 2, HEAD_DIM).transpose(1, 0, 2, 3)
    queries = projected[:, :, 0].transpose(1, 0, 2)
    head_out = lax.map(attend_head, (queries, kv_heads[:, :, 0], kv_heads[:, :, 1]))
    head_out = head_out.transpose(1, 0, 2).reshape(SEQ, D)
    attended = jnp.dot(head_out, out_full, preferred_element_type=jnp.float32)
    return (holding.astype(jnp.float32) + modulation[2] * attended).astype(jnp.bfloat16)

def final_layer(finished, time_mod, final_table, final_weight):
    shift_row = final_table[0] + time_mod[0]
    scale_row = final_table[1] + time_mod[1]
    exit_normed = (layer_norm(finished) * (1.0 + scale_row) + shift_row).astype(jnp.bfloat16)
    return jnp.dot(exit_normed, final_weight, preferred_element_type=jnp.float32).astype(jnp.bfloat16)

def reference(arriving, entering, section_start, timestep, qkv_weight, out_weight, stale_kv, layer_table, time_proj, final_table, final_weight):
    time_mod = time_vector(timestep, time_proj)
    qkv_sections = qkv_weight.reshape(SEGMENTS, D, 3 * D)
    out_sections = out_weight.reshape(SEGMENTS, D, D)
    stale_sections = stale_kv.reshape(SEGMENTS, IMAGE, 2 * D)
    slot_ids = jnp.arange(2 * SEGMENTS, dtype=jnp.int32)
    section_ids = slot_ids // 2
    lane_ids = slot_ids % 2
    table_rows = layer_table[section_start[section_ids]]
    holding = arriving
    exit_list = []
    for tick_index in range(TICKS):
        stream_ids = jnp.where(section_ids >= tick_index, 2 * (section_ids - tick_index) + lane_ids, 2 * (SEGMENTS + tick_index - 1 - section_ids) + lane_ids)
        patch_ids = (stream_ids % PATCHES).astype(jnp.int32)
        finished = lax.map(lambda packed: apply_layer(packed[0], packed[1], packed[2], packed[3], qkv_sections, out_sections, stale_sections, time_mod), (holding, table_rows, patch_ids, section_ids))
        exit_list.append(jnp.stack([final_layer(finished[2 * SEGMENTS - 2], time_mod, final_table, final_weight), final_layer(finished[2 * SEGMENTS - 1], time_mod, final_table, final_weight)]))
        holding = jnp.concatenate([entering[tick_index], finished[:-2]], axis=0)
    return (holding, jnp.stack(exit_list))
```

```python
import math

import jax
import jax.numpy as jnp
from jax import lax
from jax.sharding import PartitionSpec as P

D = 1152
FREQ = 256
TICKS = 2
PATCHES = 4
HEAD_DIM = 72


epsilon = 1e-06


def swapped(value, axis, apart):
    mask = 2**apart
    pairs = [(source, source ^ mask) for source in range(lax.axis_size(axis))]
    return lax.ppermute(value, axis, pairs)


def gathered(value, axis):
    peers = lax.axis_size(axis)
    copies = jnp.broadcast_to(value[None], (peers,) + value.shape)
    received = lax.all_to_all(copies, axis, 0, 0, tiled=True)
    return received.reshape((peers * value.shape[0],) + value.shape[1:])


def shifted(array, axis, by):
    peers = lax.axis_size(axis)
    pairs = [(i, i + by) for i in range(peers) if 0 <= i + by < peers]
    return lax.ppermute(array, axis, pairs)


def time_vector(timestep, time_proj):
    half_freq = FREQ // 2
    steps_k = jnp.arange(half_freq, dtype=jnp.float32)
    frequency = jnp.exp(-jnp.log(10000.0) * steps_k / half_freq)
    angles = timestep[0].astype(jnp.float32) * frequency
    embedding = jnp.concatenate([jnp.cos(angles), jnp.sin(angles)])
    time_feature = jax.nn.silu(embedding).astype(jnp.bfloat16)
    return jnp.dot(time_feature[None, :], time_proj, preferred_element_type=jnp.float32).reshape(
        3, D
    )


def layer_norm(values):
    widened = values.astype(jnp.float32)
    average = jnp.mean(widened, axis=-1, keepdims=True)
    centred = widened - average
    variance = jnp.mean(centred * centred, axis=-1, keepdims=True)
    return centred * lax.rsqrt(variance + epsilon)


def attend(by_head, stale_full, patch):
    seq_rows = by_head.shape[0]
    image_rows = stale_full.shape[0]
    heads_here = by_head.shape[1] // (3 * HEAD_DIM)
    unpacked = by_head.reshape(seq_rows, heads_here, 3, HEAD_DIM)
    queries = unpacked[:, :, 0]
    fresh_kv = unpacked[:, :, 1:3].reshape(seq_rows, heads_here * 2 * HEAD_DIM)
    start_row = patch * seq_rows
    kv_all = lax.dynamic_update_slice(stale_full, fresh_kv, (start_row, jnp.zeros((), jnp.int32)))
    kv_heads = kv_all.reshape(image_rows, heads_here, 2, HEAD_DIM)
    keys_all = kv_heads[:, :, 0]
    values_all = kv_heads[:, :, 1]
    block_rows = math.gcd(seq_rows, 512)
    query_blocks = queries.reshape(seq_rows // block_rows, block_rows, heads_here, HEAD_DIM)
    inverse = HEAD_DIM ** (-0.5)

    def one_block(query_block):
        scores = (
            jnp.einsum("qhe,khe->hqk", query_block, keys_all, preferred_element_type=jnp.float32)
            * inverse
        )
        weights = jnp.exp(scores - jnp.max(scores, axis=2, keepdims=True))
        probability = (weights / jnp.sum(weights, axis=2, keepdims=True)).astype(jnp.bfloat16)
        return jnp.einsum(
            "hqk,khe->qhe", probability, values_all, preferred_element_type=jnp.float32
        ).astype(jnp.bfloat16)

    blocks_out = lax.map(one_block, query_blocks)
    return blocks_out.reshape(seq_rows, heads_here * HEAD_DIM)


def finish(finished, time_mod, final_table, final_weight):
    shift_row = final_table[0] + time_mod[0]
    scale_row = final_table[1] + time_mod[1]
    exit_normed = (layer_norm(finished) * (1.0 + scale_row) + shift_row).astype(jnp.bfloat16)
    return jnp.dot(exit_normed, final_weight, preferred_element_type=jnp.float32).astype(jnp.bfloat16)


def spread_exits(exits, segment_count):
    by_column = jnp.transpose(exits, (2, 0, 1))
    received = lax.all_to_all(by_column, "segment", 0, 0, tiled=True)
    last = received[segment_count - 2 :]
    return jnp.transpose(last, (1, 0, 2))[..., None]


def body(
    arriving,
    entering,
    section_start,
    timestep,
    qkv_weight,
    out_weight,
    stale_kv,
    layer_table,
    time_proj,
    final_table,
    final_weight,
):
    segment_index = lax.axis_index("segment")
    segment_count = lax.axis_size("segment")
    section = segment_index // 2
    lane = segment_index % 2
    sections = segment_count // 2
    time_mod = time_vector(timestep, time_proj)
    table_row = lax.dynamic_index_in_dim(layer_table, section_start[section], 0, keepdims=False)
    modulation = table_row.astype(jnp.float32) + time_mod
    own_parts = (qkv_weight[0], out_weight[0], stale_kv[0])
    partner_parts = swapped((qkv_weight[0], out_weight[0], stale_kv[0]), "segment", 0)
    first_parts = [
        jnp.where(lane == 0, mine, other) for mine, other in zip(own_parts, partner_parts)
    ]
    second_parts = [
        jnp.where(lane == 0, other, mine) for mine, other in zip(own_parts, partner_parts)
    ]
    qkv_stack = jnp.stack([first_parts[0], second_parts[0]])
    out_stack = jnp.stack([first_parts[1], second_parts[1]])
    stale_full = jnp.concatenate([first_parts[2], second_parts[2]], axis=0)
    model_width = out_weight.shape[2]
    qkv_local = qkv_stack.reshape(model_width, qkv_stack.shape[2])
    out_full = jnp.transpose(gathered(jnp.transpose(out_stack, (1, 0, 2)), "blk"), (1, 0, 2))
    out_full = out_full.reshape(model_width, model_width)
    holding = arriving[0]
    exit_list = []
    for tick_index in range(TICKS):
        stream_id = jnp.where(
            section >= tick_index,
            2 * (section - tick_index) + lane,
            2 * (sections + tick_index - 1 - section) + lane,
        )
        patch = stream_id % PATCHES
        normed = (layer_norm(holding) * (1.0 + modulation[1]) + modulation[0]).astype(jnp.bfloat16)
        by_head = jnp.dot(
            gathered(normed, "blk"),
            qkv_local,
            preferred_element_type=jnp.float32,
        ).astype(jnp.bfloat16)
        head_out = attend(by_head, stale_full, patch)
        token_out = lax.all_to_all(head_out, "blk", split_axis=0, concat_axis=1, tiled=True)
        attended = jnp.dot(token_out, out_full, preferred_element_type=jnp.float32)
        finished = (holding.astype(jnp.float32) + modulation[2] * attended).astype(jnp.bfloat16)
        exit_list.append(finish(finished, time_mod, final_table, final_weight))
        passed = shifted(finished, "segment", 2)
        incoming = lax.dynamic_index_in_dim(entering[tick_index], lane, 0, keepdims=False)
        holding = jnp.where(segment_index < 2, incoming, passed)
    return (holding[None], spread_exits(jnp.stack(exit_list), segment_count))


def solution(mesh):
    in_specs = (
        P("segment", "blk", None),
        P(None, None, "blk", None),
        P(),
        P(),
        P("segment", None, "blk"),
        P("segment", "blk", None),
        P("segment", None, "blk"),
        P(),
        P(),
        P(),
        P(),
    )
    out_specs = (P("segment", "blk", None), P(None, None, "blk", "segment"))
    return jax.shard_map(body, mesh=mesh, in_specs=in_specs, out_specs=out_specs, check_vma=False)
```

```python
import math

import jax
import jax.numpy as jnp
from jax import lax
from jax.sharding import Mesh
from jax.sharding import PartitionSpec as P

D = 1152
FREQ = 256
TICKS = 2
PATCHES = 4
HEAD_DIM = 72

BLK = ("bx", "by", "bc")
SAME_CORE = ("bx", "by")
CORE = "bc"


epsilon = 1e-06


def swapped(value, axis, apart):
    mask = 2**apart
    pairs = [(source, source ^ mask) for source in range(lax.axis_size(axis))]
    return lax.ppermute(value, axis, pairs)


def core_swapped(value):
    return lax.ppermute(value, CORE, [(0, 1), (1, 0)])


def shifted(array, axis, by):
    peers = lax.axis_size(axis)
    pairs = [(i, i + by) for i in range(peers) if 0 <= i + by < peers]
    return lax.ppermute(array, axis, pairs)


def gathered_tokens(value, groups):
    copies = jnp.broadcast_to(value[None], (groups,) + value.shape)
    same_core = lax.all_to_all(copies, SAME_CORE, 0, 0, tiled=True)
    other_core = core_swapped(same_core)
    core = lax.axis_index(CORE)
    first = jnp.where(core == 0, same_core, other_core)
    second = jnp.where(core == 0, other_core, same_core)
    both = jnp.stack([first, second], axis=1)
    return both.reshape((groups * 2 * value.shape[0],) + value.shape[1:])


def scattered_sum(partial, groups):
    rows = partial.shape[0] // (groups * 2)
    parts = partial.reshape(groups, 2, rows, partial.shape[1])
    core = lax.axis_index(CORE)
    mine = jnp.where(core == 0, parts[:, 0], parts[:, 1])
    theirs = jnp.where(core == 0, parts[:, 1], parts[:, 0])
    summed = (mine + core_swapped(theirs)).astype(jnp.bfloat16)
    received = lax.all_to_all(summed, SAME_CORE, 0, 0, tiled=True)
    return jnp.sum(received.astype(jnp.float32), axis=0)


def head_rows(out_stack, heads):
    per_half = heads // 2
    pieces = []
    for parity in range(2):
        total = None
        for half in range(2):
            pairs = [(2 * k + parity, half * per_half + k) for k in range(per_half)]
            moved = lax.ppermute(out_stack[half], BLK, pairs)
            total = moved if total is None else total + moved
        pieces.append(total)
    return jnp.concatenate(pieces, axis=0)


def time_vector(timestep, time_proj):
    half_freq = FREQ // 2
    steps_k = jnp.arange(half_freq, dtype=jnp.float32)
    frequency = jnp.exp(-jnp.log(10000.0) * steps_k / half_freq)
    angles = timestep[0].astype(jnp.float32) * frequency
    embedding = jnp.concatenate([jnp.cos(angles), jnp.sin(angles)])
    time_feature = jax.nn.silu(embedding).astype(jnp.bfloat16)
    return jnp.dot(time_feature[None, :], time_proj, preferred_element_type=jnp.float32).reshape(
        3, D
    )


def layer_norm(values):
    widened = values.astype(jnp.float32)
    average = jnp.mean(widened, axis=-1, keepdims=True)
    centred = widened - average
    variance = jnp.mean(centred * centred, axis=-1, keepdims=True)
    return centred * lax.rsqrt(variance + epsilon)


def attend(by_head, stale_full, patch):
    seq_rows = by_head.shape[0]
    image_rows = stale_full.shape[0]
    heads_here = by_head.shape[1] // (3 * HEAD_DIM)
    unpacked = by_head.reshape(seq_rows, heads_here, 3, HEAD_DIM)
    queries = unpacked[:, :, 0]
    fresh_kv = unpacked[:, :, 1:3].reshape(seq_rows, heads_here * 2 * HEAD_DIM)
    start_row = patch * seq_rows
    kv_all = lax.dynamic_update_slice(stale_full, fresh_kv, (start_row, jnp.zeros((), jnp.int32)))
    kv_heads = kv_all.reshape(image_rows, heads_here, 2, HEAD_DIM)
    keys_all = kv_heads[:, :, 0]
    values_all = kv_heads[:, :, 1]
    block_rows = math.gcd(seq_rows, 512)
    query_blocks = queries.reshape(seq_rows // block_rows, block_rows, heads_here, HEAD_DIM)
    inverse = HEAD_DIM ** (-0.5)

    def one_block(query_block):
        scores = (
            jnp.einsum("qhe,khe->hqk", query_block, keys_all, preferred_element_type=jnp.float32)
            * inverse
        )
        weights = jnp.exp(scores - jnp.max(scores, axis=2, keepdims=True))
        probability = (weights / jnp.sum(weights, axis=2, keepdims=True)).astype(jnp.bfloat16)
        return jnp.einsum(
            "hqk,khe->qhe", probability, values_all, preferred_element_type=jnp.float32
        ).astype(jnp.bfloat16)

    blocks_out = lax.map(one_block, query_blocks)
    return blocks_out.reshape(seq_rows, heads_here * HEAD_DIM)


def finish(finished, time_mod, final_table, final_weight):
    shift_row = final_table[0] + time_mod[0]
    scale_row = final_table[1] + time_mod[1]
    exit_normed = (layer_norm(finished) * (1.0 + scale_row) + shift_row).astype(jnp.bfloat16)
    return jnp.dot(exit_normed, final_weight, preferred_element_type=jnp.float32).astype(jnp.bfloat16)


def spread_exits(exits, segment_count):
    by_column = jnp.transpose(exits, (2, 0, 1))
    received = lax.all_to_all(by_column, "segment", 0, 0, tiled=True)
    last = received[segment_count - 2 :]
    return jnp.transpose(last, (1, 0, 2))[..., None]


def body(
    arriving,
    entering,
    section_start,
    timestep,
    qkv_weight,
    out_weight,
    stale_kv,
    layer_table,
    time_proj,
    final_table,
    final_weight,
):
    segment_index = lax.axis_index("segment")
    segment_count = lax.axis_size("segment")
    groups = lax.axis_size("bx") * lax.axis_size("by")
    heads = groups * 2
    section = segment_index // 2
    lane = segment_index % 2
    sections = segment_count // 2
    time_mod = time_vector(timestep, time_proj)
    table_row = lax.dynamic_index_in_dim(layer_table, section_start[section], 0, keepdims=False)
    modulation = table_row.astype(jnp.float32) + time_mod
    own_parts = (qkv_weight[0], out_weight[0], stale_kv[0])
    partner_parts = swapped((qkv_weight[0], out_weight[0], stale_kv[0]), "segment", 0)
    first_parts = [
        jnp.where(lane == 0, mine, other) for mine, other in zip(own_parts, partner_parts)
    ]
    second_parts = [
        jnp.where(lane == 0, other, mine) for mine, other in zip(own_parts, partner_parts)
    ]
    qkv_stack = jnp.stack([first_parts[0], second_parts[0]])
    out_stack = jnp.stack([first_parts[1], second_parts[1]])
    stale_full = jnp.concatenate([first_parts[2], second_parts[2]], axis=0)
    model_width = out_weight.shape[2]
    qkv_local = qkv_stack.reshape(model_width, qkv_stack.shape[2])
    out_head = head_rows(out_stack, heads)
    holding = arriving[0]
    exit_list = []
    for tick_index in range(TICKS):
        stream_id = jnp.where(
            section >= tick_index,
            2 * (section - tick_index) + lane,
            2 * (sections + tick_index - 1 - section) + lane,
        )
        patch = stream_id % PATCHES
        normed = (layer_norm(holding) * (1.0 + modulation[1]) + modulation[0]).astype(jnp.bfloat16)
        by_head = jnp.dot(
            gathered_tokens(normed, groups),
            qkv_local,
            preferred_element_type=jnp.float32,
        ).astype(jnp.bfloat16)
        head_out = attend(by_head, stale_full, patch)
        partial = jnp.dot(head_out, out_head, preferred_element_type=jnp.float32)
        attended = scattered_sum(partial, groups)
        finished = (holding.astype(jnp.float32) + modulation[2] * attended).astype(jnp.bfloat16)
        exit_list.append(finish(finished, time_mod, final_table, final_weight))
        passed = shifted(finished, "segment", 2)
        incoming = lax.dynamic_index_in_dim(entering[tick_index], lane, 0, keepdims=False)
        holding = jnp.where(segment_index < 2, incoming, passed)
    return (holding[None], spread_exits(jnp.stack(exit_list), segment_count))


def solution(mesh):
    blk_size = mesh.shape["blk"]
    split = Mesh(
        mesh.devices.reshape(mesh.shape["segment"], blk_size // 4, 2, 2),
        ("segment",) + BLK,
    )
    in_specs = (
        P("segment", BLK, None),
        P(None, None, BLK, None),
        P(),
        P(),
        P("segment", None, BLK),
        P("segment", BLK, None),
        P("segment", None, BLK),
        P(),
        P(),
        P(),
        P(),
    )
    out_specs = (P("segment", BLK, None), P(None, None, BLK, "segment"))
    return jax.shard_map(body, mesh=split, in_specs=in_specs, out_specs=out_specs, check_vma=False)
```

```python
import math

import jax
import jax.numpy as jnp
from jax import lax
from jax.sharding import Mesh
from jax.sharding import PartitionSpec as P

D = 1152
FREQ = 256
TICKS = 2
PATCHES = 4
HEAD_DIM = 72

BLK = ("bx", "by", "bc")
SAME_CORE = ("bx", "by")
CORE = "bc"


epsilon = 1e-06


def swapped(value, axis, apart):
    mask = 2**apart
    pairs = [(source, source ^ mask) for source in range(lax.axis_size(axis))]
    return lax.ppermute(value, axis, pairs)


def core_swapped(value):
    return lax.ppermute(value, CORE, [(0, 1), (1, 0)])


def shifted(array, axis, by):
    peers = lax.axis_size(axis)
    pairs = [(i, i + by) for i in range(peers) if 0 <= i + by < peers]
    return lax.ppermute(array, axis, pairs)


def group_shifted(value, groups, step):
    pairs = [(i, (i + step) % groups) for i in range(groups)]
    return lax.ppermute(value, SAME_CORE, pairs)


def gathered_tokens(value, groups):
    same_core = jnp.stack([value] + [group_shifted(value, groups, k) for k in range(1, groups)])
    both = jnp.stack([same_core, core_swapped(same_core)])
    return both.reshape((2 * groups * value.shape[0],) + value.shape[1:])


def scattered_sum(partial, groups):
    parts = partial.reshape(2, groups, partial.shape[0] // (2 * groups), partial.shape[1])
    summed = (parts[0] + core_swapped(parts[1])).astype(jnp.bfloat16)
    total = summed[0].astype(jnp.float32)
    for k in range(1, groups):
        total = total + group_shifted(summed[k], groups, -k).astype(jnp.float32)
    return total


def head_rows(out_stack, heads):
    per_half = heads // 2
    pieces = []
    for parity in range(2):
        total = None
        for half in range(2):
            pairs = [(2 * k + parity, half * per_half + k) for k in range(per_half)]
            moved = lax.ppermute(out_stack[half], BLK, pairs)
            total = moved if total is None else total + moved
        pieces.append(total)
    return jnp.concatenate(pieces, axis=0)


def time_vector(timestep, time_proj):
    half_freq = FREQ // 2
    steps_k = jnp.arange(half_freq, dtype=jnp.float32)
    frequency = jnp.exp(-jnp.log(10000.0) * steps_k / half_freq)
    angles = timestep[0].astype(jnp.float32) * frequency
    embedding = jnp.concatenate([jnp.cos(angles), jnp.sin(angles)])
    time_feature = jax.nn.silu(embedding).astype(jnp.bfloat16)
    return jnp.dot(time_feature[None, :], time_proj, preferred_element_type=jnp.float32).reshape(
        3, D
    )


def layer_norm(values):
    widened = values.astype(jnp.float32)
    average = jnp.mean(widened, axis=-1, keepdims=True)
    centred = widened - average
    variance = jnp.mean(centred * centred, axis=-1, keepdims=True)
    return centred * lax.rsqrt(variance + epsilon)


def attend(by_head, stale_full, patch):
    seq_rows = by_head.shape[0]
    image_rows = stale_full.shape[0]
    heads_here = by_head.shape[1] // (3 * HEAD_DIM)
    unpacked = by_head.reshape(seq_rows, heads_here, 3, HEAD_DIM)
    queries = unpacked[:, :, 0]
    fresh_kv = unpacked[:, :, 1:3].reshape(seq_rows, heads_here * 2 * HEAD_DIM)
    start_row = patch * seq_rows
    kv_all = lax.dynamic_update_slice(stale_full, fresh_kv, (start_row, jnp.zeros((), jnp.int32)))
    kv_heads = kv_all.reshape(image_rows, heads_here, 2, HEAD_DIM)
    keys_all = kv_heads[:, :, 0]
    values_all = kv_heads[:, :, 1]
    block_rows = math.gcd(seq_rows, 512)
    query_blocks = queries.reshape(seq_rows // block_rows, block_rows, heads_here, HEAD_DIM)
    inverse = HEAD_DIM ** (-0.5)

    def one_block(query_block):
        scores = (
            jnp.einsum("qhe,khe->hqk", query_block, keys_all, preferred_element_type=jnp.float32)
            * inverse
        )
        weights = jnp.exp(scores - jnp.max(scores, axis=2, keepdims=True))
        probability = (weights / jnp.sum(weights, axis=2, keepdims=True)).astype(jnp.bfloat16)
        return jnp.einsum(
            "hqk,khe->qhe", probability, values_all, preferred_element_type=jnp.float32
        ).astype(jnp.bfloat16)

    blocks_out = lax.map(one_block, query_blocks)
    return blocks_out.reshape(seq_rows, heads_here * HEAD_DIM)


def finish(finished, time_mod, final_table, final_weight):
    shift_row = final_table[0] + time_mod[0]
    scale_row = final_table[1] + time_mod[1]
    exit_normed = (layer_norm(finished) * (1.0 + scale_row) + shift_row).astype(jnp.bfloat16)
    return jnp.dot(exit_normed, final_weight, preferred_element_type=jnp.float32).astype(jnp.bfloat16)


def spread_exits(exits, segment_count):
    by_column = jnp.transpose(exits, (2, 0, 1))
    received = lax.all_to_all(by_column, "segment", 0, 0, tiled=True)
    last = received[segment_count - 2 :]
    return jnp.transpose(last, (1, 0, 2))[..., None]


def body(
    arriving,
    entering,
    section_start,
    timestep,
    qkv_weight,
    out_weight,
    stale_kv,
    layer_table,
    time_proj,
    final_table,
    final_weight,
):
    segment_index = lax.axis_index("segment")
    segment_count = lax.axis_size("segment")
    groups = lax.axis_size("bx") * lax.axis_size("by")
    heads = groups * 2
    section = segment_index // 2
    lane = segment_index % 2
    sections = segment_count // 2
    time_mod = time_vector(timestep, time_proj)
    table_row = lax.dynamic_index_in_dim(layer_table, section_start[section], 0, keepdims=False)
    modulation = table_row.astype(jnp.float32) + time_mod
    own_parts = (qkv_weight[0], out_weight[0], stale_kv[0])
    partner_parts = swapped((qkv_weight[0], out_weight[0], stale_kv[0]), "segment", 0)
    first_parts = [
        jnp.where(lane == 0, mine, other) for mine, other in zip(own_parts, partner_parts)
    ]
    second_parts = [
        jnp.where(lane == 0, other, mine) for mine, other in zip(own_parts, partner_parts)
    ]
    qkv_stack = jnp.stack([first_parts[0], second_parts[0]])
    out_stack = jnp.stack([first_parts[1], second_parts[1]])
    stale_full = jnp.concatenate([first_parts[2], second_parts[2]], axis=0)
    model_width = out_weight.shape[2]
    qkv_local = qkv_stack.reshape(model_width, qkv_stack.shape[2])
    out_head = head_rows(out_stack, heads)
    holding = arriving[0]
    exit_list = []
    for tick_index in range(TICKS):
        stream_id = jnp.where(
            section >= tick_index,
            2 * (section - tick_index) + lane,
            2 * (sections + tick_index - 1 - section) + lane,
        )
        patch = stream_id % PATCHES
        normed = (layer_norm(holding) * (1.0 + modulation[1]) + modulation[0]).astype(jnp.bfloat16)
        by_head = jnp.dot(
            gathered_tokens(normed, groups),
            qkv_local,
            preferred_element_type=jnp.float32,
        ).astype(jnp.bfloat16)
        head_out = attend(by_head, stale_full, patch)
        partial = jnp.dot(head_out, out_head, preferred_element_type=jnp.float32)
        attended = scattered_sum(partial, groups)
        finished = (holding.astype(jnp.float32) + modulation[2] * attended).astype(jnp.bfloat16)
        exit_list.append(finish(finished, time_mod, final_table, final_weight))
        passed = shifted(finished, "segment", 2)
        incoming = lax.dynamic_index_in_dim(entering[tick_index], lane, 0, keepdims=False)
        holding = jnp.where(segment_index < 2, incoming, passed)
    return (holding[None], spread_exits(jnp.stack(exit_list), segment_count))


def solution(mesh):
    blk_size = mesh.shape["blk"]
    split = Mesh(
        mesh.devices.reshape(mesh.shape["segment"], blk_size // 4, 2, 2),
        ("segment",) + BLK,
    )
    in_specs = (
        P("segment", BLK, None),
        P(None, None, BLK, None),
        P(),
        P(),
        P("segment", None, BLK),
        P("segment", BLK, None),
        P("segment", None, BLK),
        P(),
        P(),
        P(),
        P(),
    )
    out_specs = (P("segment", BLK, None), P(None, None, BLK, "segment"))
    return jax.shard_map(body, mesh=split, in_specs=in_specs, out_specs=out_specs, check_vma=False)
```

```python
import math

import jax
import jax.numpy as jnp
from jax import lax
from jax.sharding import Mesh
from jax.sharding import PartitionSpec as P

D = 1152
FREQ = 256
TICKS = 2
PATCHES = 4
HEAD_DIM = 72

BLK = ("xh", "xl", "by", "bc")
GATHER_ORDER = ("by", "xh", "xl", "bc")


epsilon = 1e-06


def swapped(value, axis, apart):
    mask = 2**apart
    pairs = [(source, source ^ mask) for source in range(lax.axis_size(axis))]
    return lax.ppermute(value, axis, pairs)


def pair_swapped(value, axis):
    return lax.ppermute(value, axis, [(0, 1), (1, 0)])


def shifted(array, axis, by):
    peers = lax.axis_size(axis)
    pairs = [(i, i + by) for i in range(peers) if 0 <= i + by < peers]
    return lax.ppermute(array, axis, pairs)


def gathered_tokens(value):
    held = value
    for axis in GATHER_ORDER:
        held = jnp.stack([held, pair_swapped(held, axis)])
    return held.reshape((-1,) + value.shape[1:])


def scattered_sum(partial):
    shape = (2,) * len(GATHER_ORDER) + (-1, partial.shape[1])
    held = partial.reshape(shape)
    for step, axis in enumerate(reversed(GATHER_ORDER)):
        sent = held[1] if step == 0 else held[1].astype(jnp.bfloat16)
        held = held[0] + pair_swapped(sent, axis).astype(jnp.float32)
    return held


def head_rows(out_rows, heads):
    segment_index = lax.axis_index("segment")
    lane = segment_index % 2
    per_half = heads // 2
    segments = lax.axis_size("segment")
    moved = []
    for flip in range(2):
        pairs = []
        for segment in range(segments):
            for j in range(heads):
                source_lane = segment % 2
                target_lane = (j % 2) ^ flip
                target = (segment - source_lane + target_lane) * heads + source_lane * per_half + j // 2
                pairs.append((segment * heads + j, target))
        moved.append(lax.ppermute(out_rows, ("segment",) + BLK, pairs))
    first = jnp.where(lane == 0, moved[0], moved[1])
    second = jnp.where(lane == 0, moved[1], moved[0])
    return jnp.concatenate([first, second], axis=0)


def time_vector(timestep, time_proj):
    half_freq = FREQ // 2
    steps_k = jnp.arange(half_freq, dtype=jnp.float32)
    frequency = jnp.exp(-jnp.log(10000.0) * steps_k / half_freq)
    angles = timestep[0].astype(jnp.float32) * frequency
    embedding = jnp.concatenate([jnp.cos(angles), jnp.sin(angles)])
    time_feature = jax.nn.silu(embedding).astype(jnp.bfloat16)
    return jnp.dot(time_feature[None, :], time_proj, preferred_element_type=jnp.float32).reshape(
        3, D
    )


def layer_norm(values):
    widened = values.astype(jnp.float32)
    average = jnp.mean(widened, axis=-1, keepdims=True)
    centred = widened - average
    variance = jnp.mean(centred * centred, axis=-1, keepdims=True)
    return centred * lax.rsqrt(variance + epsilon)


def attend(by_head, stale_full, patch):
    seq_rows = by_head.shape[0]
    image_rows = stale_full.shape[0]
    heads_here = by_head.shape[1] // (3 * HEAD_DIM)
    unpacked = by_head.reshape(seq_rows, heads_here, 3, HEAD_DIM)
    queries = unpacked[:, :, 0]
    fresh_kv = unpacked[:, :, 1:3].reshape(seq_rows, heads_here * 2 * HEAD_DIM)
    start_row = patch * seq_rows
    kv_all = lax.dynamic_update_slice(stale_full, fresh_kv, (start_row, jnp.zeros((), jnp.int32)))
    kv_heads = kv_all.reshape(image_rows, heads_here, 2, HEAD_DIM)
    keys_all = kv_heads[:, :, 0]
    values_all = kv_heads[:, :, 1]
    block_rows = math.gcd(seq_rows, 512)
    query_blocks = queries.reshape(seq_rows // block_rows, block_rows, heads_here, HEAD_DIM)
    inverse = HEAD_DIM ** (-0.5)

    def one_block(query_block):
        scores = (
            jnp.einsum("qhe,khe->hqk", query_block, keys_all, preferred_element_type=jnp.float32)
            * inverse
        )
        weights = jnp.exp(scores - jnp.max(scores, axis=2, keepdims=True))
        probability = (weights / jnp.sum(weights, axis=2, keepdims=True)).astype(jnp.bfloat16)
        return jnp.einsum(
            "hqk,khe->qhe", probability, values_all, preferred_element_type=jnp.float32
        ).astype(jnp.bfloat16)

    blocks_out = lax.map(one_block, query_blocks)
    return blocks_out.reshape(seq_rows, heads_here * HEAD_DIM)


def finish(finished, time_mod, final_table, final_weight):
    shift_row = final_table[0] + time_mod[0]
    scale_row = final_table[1] + time_mod[1]
    exit_normed = (layer_norm(finished) * (1.0 + scale_row) + shift_row).astype(jnp.bfloat16)
    return jnp.dot(exit_normed, final_weight, preferred_element_type=jnp.float32).astype(jnp.bfloat16)


def spread_exits(exits, segment_count):
    by_column = jnp.transpose(exits, (2, 0, 1))
    received = lax.all_to_all(by_column, "segment", 0, 0, tiled=True)
    last = received[segment_count - 2 :]
    return jnp.transpose(last, (1, 0, 2))[..., None]


def body(
    arriving,
    entering,
    section_start,
    timestep,
    qkv_weight,
    out_weight,
    stale_kv,
    layer_table,
    time_proj,
    final_table,
    final_weight,
):
    segment_index = lax.axis_index("segment")
    segment_count = lax.axis_size("segment")
    heads = 2 ** len(BLK)
    section = segment_index // 2
    lane = segment_index % 2
    sections = segment_count // 2
    time_mod = time_vector(timestep, time_proj)
    table_row = lax.dynamic_index_in_dim(layer_table, section_start[section], 0, keepdims=False)
    modulation = table_row.astype(jnp.float32) + time_mod
    own_qkv, own_stale = qkv_weight[0], stale_kv[0]
    packed = jnp.concatenate([own_qkv.reshape(-1), own_stale.reshape(-1)])
    partner = swapped(packed, "segment", 0)
    partner_qkv = partner[: own_qkv.size].reshape(own_qkv.shape)
    partner_stale = partner[own_qkv.size :].reshape(own_stale.shape)
    qkv_first = jnp.where(lane == 0, own_qkv, partner_qkv)
    qkv_second = jnp.where(lane == 0, partner_qkv, own_qkv)
    stale_first = jnp.where(lane == 0, own_stale, partner_stale)
    stale_second = jnp.where(lane == 0, partner_stale, own_stale)
    qkv_local = jnp.concatenate([qkv_first, qkv_second], axis=0)
    stale_full = jnp.concatenate([stale_first, stale_second], axis=0)
    out_head = head_rows(out_weight[0], heads)
    holding = arriving[0]
    exit_list = []
    for tick_index in range(TICKS):
        stream_id = jnp.where(
            section >= tick_index,
            2 * (section - tick_index) + lane,
            2 * (sections + tick_index - 1 - section) + lane,
        )
        patch = stream_id % PATCHES
        normed = (layer_norm(holding) * (1.0 + modulation[1]) + modulation[0]).astype(jnp.bfloat16)
        by_head = jnp.dot(
            gathered_tokens(normed),
            qkv_local,
            preferred_element_type=jnp.float32,
        ).astype(jnp.bfloat16)
        head_out = attend(by_head, stale_full, patch)
        partial = jnp.dot(head_out, out_head, preferred_element_type=jnp.float32)
        attended = scattered_sum(partial)
        finished = (holding.astype(jnp.float32) + modulation[2] * attended).astype(jnp.bfloat16)
        exit_list.append(finish(finished, time_mod, final_table, final_weight))
        passed = shifted(finished, "segment", 2)
        incoming = lax.dynamic_index_in_dim(entering[tick_index], lane, 0, keepdims=False)
        holding = jnp.where(segment_index < 2, incoming, passed)
    return (holding[None], spread_exits(jnp.stack(exit_list), segment_count))


def solution(mesh):
    blk_size = mesh.shape["blk"]
    split = Mesh(
        mesh.devices.reshape(mesh.shape["segment"], blk_size // 8, 2, 2, 2),
        ("segment",) + BLK,
    )
    in_specs = (
        P("segment", BLK, None),
        P(None, None, BLK, None),
        P(),
        P(),
        P("segment", None, BLK),
        P("segment", BLK, None),
        P("segment", None, BLK),
        P(),
        P(),
        P(),
        P(),
    )
    out_specs = (P("segment", BLK, None), P(None, None, BLK, "segment"))
    return jax.shard_map(body, mesh=split, in_specs=in_specs, out_specs=out_specs, check_vma=False)
```

```python
import math

import jax
import jax.numpy as jnp
from jax import lax
from jax.sharding import Mesh
from jax.sharding import PartitionSpec as P

D = 1152
FREQ = 256
TICKS = 2
PATCHES = 4
HEAD_DIM = 72

BLK = ("bx", "by", "bc")
SAME_CORE = ("bx", "by")
CORE = "bc"


epsilon = 1e-06


def swapped(value, axis, apart):
    mask = 2**apart
    pairs = [(source, source ^ mask) for source in range(lax.axis_size(axis))]
    return lax.ppermute(value, axis, pairs)


def core_swapped(value):
    return lax.ppermute(value, CORE, [(0, 1), (1, 0)])


def shifted(array, axis, by):
    peers = lax.axis_size(axis)
    pairs = [(i, i + by) for i in range(peers) if 0 <= i + by < peers]
    return lax.ppermute(array, axis, pairs)


def gathered_tokens(value, groups):
    copies = jnp.broadcast_to(value[None], (groups,) + value.shape)
    same_core = lax.all_to_all(copies, SAME_CORE, 0, 0, tiled=True)
    other_core = core_swapped(same_core)
    core = lax.axis_index(CORE)
    first = jnp.where(core == 0, same_core, other_core)
    second = jnp.where(core == 0, other_core, same_core)
    both = jnp.stack([first, second], axis=1)
    return both.reshape((groups * 2 * value.shape[0],) + value.shape[1:])


def scattered_sum(partial):
    heads = lax.axis_size(BLK)
    chunks = partial.astype(jnp.bfloat16).reshape(heads, -1, partial.shape[1])
    received = lax.all_to_all(chunks, BLK, 0, 0, tiled=True)
    return jnp.sum(received.astype(jnp.float32), axis=0)


def head_rows(out_rows, heads):
    segment_index = lax.axis_index("segment")
    lane = segment_index % 2
    per_half = heads // 2
    segments = lax.axis_size("segment")
    moved = []
    for flip in range(2):
        pairs = []
        for segment in range(segments):
            for j in range(heads):
                source_lane = segment % 2
                target_lane = (j % 2) ^ flip
                target = (segment - source_lane + target_lane) * heads + source_lane * per_half + j // 2
                pairs.append((segment * heads + j, target))
        moved.append(lax.ppermute(out_rows, ("segment",) + BLK, pairs))
    first = jnp.where(lane == 0, moved[0], moved[1])
    second = jnp.where(lane == 0, moved[1], moved[0])
    return jnp.concatenate([first, second], axis=0)


def time_vector(timestep, time_proj):
    half_freq = FREQ // 2
    steps_k = jnp.arange(half_freq, dtype=jnp.float32)
    frequency = jnp.exp(-jnp.log(10000.0) * steps_k / half_freq)
    angles = timestep[0].astype(jnp.float32) * frequency
    embedding = jnp.concatenate([jnp.cos(angles), jnp.sin(angles)])
    time_feature = jax.nn.silu(embedding).astype(jnp.bfloat16)
    return jnp.dot(time_feature[None, :], time_proj, preferred_element_type=jnp.float32).reshape(
        3, D
    )


def layer_norm(values):
    widened = values.astype(jnp.float32)
    average = jnp.mean(widened, axis=-1, keepdims=True)
    centred = widened - average
    variance = jnp.mean(centred * centred, axis=-1, keepdims=True)
    return centred * lax.rsqrt(variance + epsilon)


def attend(by_head, stale_full, patch):
    seq_rows = by_head.shape[0]
    image_rows = stale_full.shape[0]
    heads_here = by_head.shape[1] // (3 * HEAD_DIM)
    unpacked = by_head.reshape(seq_rows, heads_here, 3, HEAD_DIM)
    queries = unpacked[:, :, 0]
    fresh_kv = unpacked[:, :, 1:3].reshape(seq_rows, heads_here * 2 * HEAD_DIM)
    start_row = patch * seq_rows
    kv_all = lax.dynamic_update_slice(stale_full, fresh_kv, (start_row, jnp.zeros((), jnp.int32)))
    kv_heads = kv_all.reshape(image_rows, heads_here, 2, HEAD_DIM)
    keys_all = kv_heads[:, :, 0]
    values_all = kv_heads[:, :, 1]
    block_rows = math.gcd(seq_rows, 512)
    query_blocks = queries.reshape(seq_rows // block_rows, block_rows, heads_here, HEAD_DIM)
    inverse = HEAD_DIM ** (-0.5)

    def one_block(query_block):
        scores = (
            jnp.einsum("qhe,khe->hqk", query_block, keys_all, preferred_element_type=jnp.float32)
            * inverse
        )
        weights = jnp.exp(scores - jnp.max(scores, axis=2, keepdims=True))
        probability = (weights / jnp.sum(weights, axis=2, keepdims=True)).astype(jnp.bfloat16)
        return jnp.einsum(
            "hqk,khe->qhe", probability, values_all, preferred_element_type=jnp.float32
        ).astype(jnp.bfloat16)

    blocks_out = lax.map(one_block, query_blocks)
    return blocks_out.reshape(seq_rows, heads_here * HEAD_DIM)


def finish(finished, time_mod, final_table, final_weight):
    shift_row = final_table[0] + time_mod[0]
    scale_row = final_table[1] + time_mod[1]
    exit_normed = (layer_norm(finished) * (1.0 + scale_row) + shift_row).astype(jnp.bfloat16)
    return jnp.dot(exit_normed, final_weight, preferred_element_type=jnp.float32).astype(jnp.bfloat16)


def spread_exits(exits, segment_count):
    by_column = jnp.transpose(exits, (2, 0, 1))
    received = lax.all_to_all(by_column, "segment", 0, 0, tiled=True)
    last = received[segment_count - 2 :]
    return jnp.transpose(last, (1, 0, 2))[..., None]


def body(
    arriving,
    entering,
    section_start,
    timestep,
    qkv_weight,
    out_weight,
    stale_kv,
    layer_table,
    time_proj,
    final_table,
    final_weight,
):
    segment_index = lax.axis_index("segment")
    segment_count = lax.axis_size("segment")
    groups = lax.axis_size("bx") * lax.axis_size("by")
    heads = groups * 2
    section = segment_index // 2
    lane = segment_index % 2
    sections = segment_count // 2
    time_mod = time_vector(timestep, time_proj)
    table_row = lax.dynamic_index_in_dim(layer_table, section_start[section], 0, keepdims=False)
    modulation = table_row.astype(jnp.float32) + time_mod
    own_parts = (qkv_weight[0], stale_kv[0])
    partner_parts = swapped(own_parts, "segment", 0)
    first_parts = [
        jnp.where(lane == 0, mine, other) for mine, other in zip(own_parts, partner_parts)
    ]
    second_parts = [
        jnp.where(lane == 0, other, mine) for mine, other in zip(own_parts, partner_parts)
    ]
    qkv_local = jnp.concatenate([first_parts[0], second_parts[0]], axis=0)
    stale_full = jnp.concatenate([first_parts[1], second_parts[1]], axis=0)
    out_head = head_rows(out_weight[0], heads)
    holding = arriving[0]
    exit_list = []
    for tick_index in range(TICKS):
        stream_id = jnp.where(
            section >= tick_index,
            2 * (section - tick_index) + lane,
            2 * (sections + tick_index - 1 - section) + lane,
        )
        patch = stream_id % PATCHES
        normed = (layer_norm(holding) * (1.0 + modulation[1]) + modulation[0]).astype(jnp.bfloat16)
        by_head = jnp.dot(
            gathered_tokens(normed, groups),
            qkv_local,
            preferred_element_type=jnp.float32,
        ).astype(jnp.bfloat16)
        head_out = attend(by_head, stale_full, patch)
        partial = jnp.dot(head_out, out_head, preferred_element_type=jnp.float32)
        attended = scattered_sum(partial)
        finished = (holding.astype(jnp.float32) + modulation[2] * attended).astype(jnp.bfloat16)
        exit_list.append(finish(finished, time_mod, final_table, final_weight))
        passed = shifted(finished, "segment", 2)
        incoming = lax.dynamic_index_in_dim(entering[tick_index], lane, 0, keepdims=False)
        holding = jnp.where(segment_index < 2, incoming, passed)
    return (holding[None], spread_exits(jnp.stack(exit_list), segment_count))


def solution(mesh):
    blk_size = mesh.shape["blk"]
    split = Mesh(
        mesh.devices.reshape(mesh.shape["segment"], blk_size // 4, 2, 2),
        ("segment",) + BLK,
    )
    in_specs = (
        P("segment", BLK, None),
        P(None, None, BLK, None),
        P(),
        P(),
        P("segment", None, BLK),
        P("segment", BLK, None),
        P("segment", None, BLK),
        P(),
        P(),
        P(),
        P(),
    )
    out_specs = (P("segment", BLK, None), P(None, None, BLK, "segment"))
    return jax.shard_map(body, mesh=split, in_specs=in_specs, out_specs=out_specs, check_vma=False)
```

```python
import math

import jax
import jax.numpy as jnp
from jax import lax
from jax.sharding import Mesh
from jax.sharding import PartitionSpec as P

D = 1152
FREQ = 256
TICKS = 2
PATCHES = 4
HEAD_DIM = 72

BLK = ("bx", "by", "bc")
SAME_CORE = ("bx", "by")
CORE = "bc"


epsilon = 1e-06


def swapped(value, axis, apart):
    mask = 2**apart
    pairs = [(source, source ^ mask) for source in range(lax.axis_size(axis))]
    return lax.ppermute(value, axis, pairs)


def core_swapped(value):
    return lax.ppermute(value, CORE, [(0, 1), (1, 0)])


def shifted(array, axis, by):
    peers = lax.axis_size(axis)
    pairs = [(i, i + by) for i in range(peers) if 0 <= i + by < peers]
    return lax.ppermute(array, axis, pairs)


def gathered_tokens(value, groups):
    copies = jnp.broadcast_to(value[None], (groups,) + value.shape)
    same_core = lax.all_to_all(copies, SAME_CORE, 0, 0, tiled=True)
    other_core = core_swapped(same_core)
    core = lax.axis_index(CORE)
    first = jnp.where(core == 0, same_core, other_core)
    second = jnp.where(core == 0, other_core, same_core)
    both = jnp.stack([first, second], axis=1)
    return both.reshape((groups * 2 * value.shape[0],) + value.shape[1:])


def scattered_sum(partial, groups):
    rows = partial.shape[0] // (groups * 2)
    parts = partial.reshape(groups, 2, rows, partial.shape[1])
    core = lax.axis_index(CORE)
    mine = jnp.where(core == 0, parts[:, 0], parts[:, 1])
    theirs = jnp.where(core == 0, parts[:, 1], parts[:, 0])
    summed = (mine + core_swapped(theirs)).astype(jnp.bfloat16)
    received = lax.all_to_all(summed, SAME_CORE, 0, 0, tiled=True)
    return jnp.sum(received.astype(jnp.float32), axis=0)


def head_rows(out_rows, heads):
    segment_index = lax.axis_index("segment")
    lane = segment_index % 2
    per_half = heads // 2
    segments = lax.axis_size("segment")
    moved = []
    for flip in range(2):
        pairs = []
        for segment in range(segments):
            for j in range(heads):
                source_lane = segment % 2
                target_lane = (j % 2) ^ flip
                target = (segment - source_lane + target_lane) * heads + source_lane * per_half + j // 2
                pairs.append((segment * heads + j, target))
        moved.append(lax.ppermute(out_rows, ("segment",) + BLK, pairs))
    first = jnp.where(lane == 0, moved[0], moved[1])
    second = jnp.where(lane == 0, moved[1], moved[0])
    return jnp.concatenate([first, second], axis=0)


def time_vector(timestep, time_proj):
    half_freq = FREQ // 2
    steps_k = jnp.arange(half_freq, dtype=jnp.float32)
    frequency = jnp.exp(-jnp.log(10000.0) * steps_k / half_freq)
    angles = timestep[0].astype(jnp.float32) * frequency
    embedding = jnp.concatenate([jnp.cos(angles), jnp.sin(angles)])
    time_feature = jax.nn.silu(embedding).astype(jnp.bfloat16)
    return jnp.dot(time_feature[None, :], time_proj, preferred_element_type=jnp.float32).reshape(
        3, D
    )


def layer_norm(values):
    widened = values.astype(jnp.float32)
    average = jnp.mean(widened, axis=-1, keepdims=True)
    centred = widened - average
    variance = jnp.mean(centred * centred, axis=-1, keepdims=True)
    return centred * lax.rsqrt(variance + epsilon)


def attend(by_head, stale_full, patch):
    seq_rows = by_head.shape[0]
    image_rows = stale_full.shape[0]
    heads_here = by_head.shape[1] // (3 * HEAD_DIM)
    unpacked = by_head.reshape(seq_rows, heads_here, 3, HEAD_DIM)
    queries = unpacked[:, :, 0]
    fresh_kv = unpacked[:, :, 1:3].reshape(seq_rows, heads_here * 2 * HEAD_DIM)
    start_row = patch * seq_rows
    kv_all = lax.dynamic_update_slice(stale_full, fresh_kv, (start_row, jnp.zeros((), jnp.int32)))
    kv_heads = kv_all.reshape(image_rows, heads_here, 2, HEAD_DIM)
    keys_all = kv_heads[:, :, 0]
    values_all = kv_heads[:, :, 1]
    block_rows = math.gcd(seq_rows, 512)
    query_blocks = queries.reshape(seq_rows // block_rows, block_rows, heads_here, HEAD_DIM)
    inverse = HEAD_DIM ** (-0.5)

    def one_block(query_block):
        scores = (
            jnp.einsum("qhe,khe->hqk", query_block, keys_all, preferred_element_type=jnp.float32)
            * inverse
        )
        weights = jnp.exp(scores - jnp.max(scores, axis=2, keepdims=True))
        probability = (weights / jnp.sum(weights, axis=2, keepdims=True)).astype(jnp.bfloat16)
        return jnp.einsum(
            "hqk,khe->qhe", probability, values_all, preferred_element_type=jnp.float32
        ).astype(jnp.bfloat16)

    blocks_out = lax.map(one_block, query_blocks)
    return blocks_out.reshape(seq_rows, heads_here * HEAD_DIM)


def finish(finished, time_mod, final_table, final_weight):
    shift_row = final_table[0] + time_mod[0]
    scale_row = final_table[1] + time_mod[1]
    exit_normed = (layer_norm(finished) * (1.0 + scale_row) + shift_row).astype(jnp.bfloat16)
    return jnp.dot(exit_normed, final_weight, preferred_element_type=jnp.float32).astype(jnp.bfloat16)


def spread_exits(exits, segment_count):
    by_column = jnp.transpose(exits, (2, 0, 1))
    received = lax.all_to_all(by_column, "segment", 0, 0, tiled=True)
    last = received[segment_count - 2 :]
    return jnp.transpose(last, (1, 0, 2))[..., None]


def body(
    arriving,
    entering,
    section_start,
    timestep,
    qkv_weight,
    out_weight,
    stale_kv,
    layer_table,
    time_proj,
    final_table,
    final_weight,
):
    segment_index = lax.axis_index("segment")
    segment_count = lax.axis_size("segment")
    groups = lax.axis_size("bx") * lax.axis_size("by")
    heads = groups * 2
    section = segment_index // 2
    lane = segment_index % 2
    sections = segment_count // 2
    time_mod = time_vector(timestep, time_proj)
    table_row = lax.dynamic_index_in_dim(layer_table, section_start[section], 0, keepdims=False)
    modulation = table_row.astype(jnp.float32) + time_mod
    own_parts = (qkv_weight[0], stale_kv[0])
    partner_parts = swapped(own_parts, "segment", 0)
    first_parts = [
        jnp.where(lane == 0, mine, other) for mine, other in zip(own_parts, partner_parts)
    ]
    second_parts = [
        jnp.where(lane == 0, other, mine) for mine, other in zip(own_parts, partner_parts)
    ]
    qkv_local = jnp.concatenate([first_parts[0], second_parts[0]], axis=0)
    stale_full = jnp.concatenate([first_parts[1], second_parts[1]], axis=0)
    out_head = head_rows(out_weight[0], heads)
    holding = arriving[0]
    exit_list = []
    for tick_index in range(TICKS):
        stream_id = jnp.where(
            section >= tick_index,
            2 * (section - tick_index) + lane,
            2 * (sections + tick_index - 1 - section) + lane,
        )
        patch = stream_id % PATCHES
        normed = (layer_norm(holding) * (1.0 + modulation[1]) + modulation[0]).astype(jnp.bfloat16)
        by_head = jnp.dot(
            gathered_tokens(normed, groups),
            qkv_local,
            preferred_element_type=jnp.float32,
        ).astype(jnp.bfloat16)
        head_out = attend(by_head, stale_full, patch)
        partial = jnp.dot(head_out, out_head, preferred_element_type=jnp.float32)
        attended = scattered_sum(partial, groups)
        finished = (holding.astype(jnp.float32) + modulation[2] * attended).astype(jnp.bfloat16)
        exit_list.append(finish(finished, time_mod, final_table, final_weight))
        passed = shifted(finished, "segment", 2)
        incoming = lax.dynamic_index_in_dim(entering[tick_index], lane, 0, keepdims=False)
        holding = jnp.where(segment_index < 2, incoming, passed)
    return (holding[None], spread_exits(jnp.stack(exit_list), segment_count))


def solution(mesh):
    blk_size = mesh.shape["blk"]
    split = Mesh(
        mesh.devices.reshape(mesh.shape["segment"], blk_size // 4, 2, 2),
        ("segment",) + BLK,
    )
    in_specs = (
        P("segment", BLK, None),
        P(None, None, BLK, None),
        P(),
        P(),
        P("segment", None, BLK),
        P("segment", BLK, None),
        P("segment", None, BLK),
        P(),
        P(),
        P(),
        P(),
    )
    out_specs = (P("segment", BLK, None), P(None, None, BLK, "segment"))
    return jax.shard_map(body, mesh=split, in_specs=in_specs, out_specs=out_specs, check_vma=False)
```

```python
import math

import jax
import jax.numpy as jnp
from jax import lax
from jax.sharding import Mesh
from jax.sharding import PartitionSpec as P

D = 1152
FREQ = 256
TICKS = 2
PATCHES = 4
HEAD_DIM = 72

BLK = ("bx", "by", "bc")
SAME_CORE = ("bx", "by")
CORE = "bc"


epsilon = 1e-06


def swapped(value, axis, apart):
    mask = 2**apart
    pairs = [(source, source ^ mask) for source in range(lax.axis_size(axis))]
    return lax.ppermute(value, axis, pairs)


def core_swapped(value):
    return lax.ppermute(value, CORE, [(0, 1), (1, 0)])


def shifted(array, axis, by):
    peers = lax.axis_size(axis)
    pairs = [(i, i + by) for i in range(peers) if 0 <= i + by < peers]
    return lax.ppermute(array, axis, pairs)


def gathered_tokens(value, groups):
    copies = jnp.broadcast_to(value[None], (groups,) + value.shape)
    same_core = lax.all_to_all(copies, SAME_CORE, 0, 0, tiled=True)
    other_core = core_swapped(same_core)
    core = lax.axis_index(CORE)
    first = jnp.where(core == 0, same_core, other_core)
    second = jnp.where(core == 0, other_core, same_core)
    both = jnp.stack([first, second], axis=1)
    return both.reshape((groups * 2 * value.shape[0],) + value.shape[1:])


def scattered_sum(partial, groups):
    rows = partial.shape[0] // (groups * 2)
    parts = partial.reshape(groups, 2, rows, partial.shape[1])
    core = lax.axis_index(CORE)
    mine = jnp.where(core == 0, parts[:, 0], parts[:, 1])
    theirs = jnp.where(core == 0, parts[:, 1], parts[:, 0])
    summed = (mine + core_swapped(theirs)).astype(jnp.bfloat16)
    received = lax.all_to_all(summed, SAME_CORE, 0, 0, tiled=True)
    return jnp.sum(received.astype(jnp.float32), axis=0)


def head_rows(out_rows, heads):
    segment_index = lax.axis_index("segment")
    lane = segment_index % 2
    per_half = heads // 2
    segments = lax.axis_size("segment")
    moved = []
    for flip in range(2):
        pairs = []
        for segment in range(segments):
            for j in range(heads):
                source_lane = segment % 2
                target_lane = (j % 2) ^ flip
                target = (segment - source_lane + target_lane) * heads + source_lane * per_half + j // 2
                pairs.append((segment * heads + j, target))
        moved.append(lax.ppermute(out_rows, ("segment",) + BLK, pairs))
    first = jnp.where(lane == 0, moved[0], moved[1])
    second = jnp.where(lane == 0, moved[1], moved[0])
    return jnp.concatenate([first, second], axis=0)


def time_vector(timestep, time_proj):
    half_freq = FREQ // 2
    steps_k = jnp.arange(half_freq, dtype=jnp.float32)
    frequency = jnp.exp(-jnp.log(10000.0) * steps_k / half_freq)
    angles = timestep[0].astype(jnp.float32) * frequency
    embedding = jnp.concatenate([jnp.cos(angles), jnp.sin(angles)])
    time_feature = jax.nn.silu(embedding).astype(jnp.bfloat16)
    return jnp.dot(time_feature[None, :], time_proj, preferred_element_type=jnp.float32).reshape(
        3, D
    )


def layer_norm(values):
    widened = values.astype(jnp.float32)
    average = jnp.mean(widened, axis=-1, keepdims=True)
    centred = widened - average
    variance = jnp.mean(centred * centred, axis=-1, keepdims=True)
    return centred * lax.rsqrt(variance + epsilon)


def attend(by_head, stale_full, patch):
    seq_rows = by_head.shape[0]
    image_rows = stale_full.shape[0]
    heads_here = by_head.shape[1] // (3 * HEAD_DIM)
    unpacked = by_head.reshape(seq_rows, heads_here, 3, HEAD_DIM)
    queries = unpacked[:, :, 0]
    fresh_kv = unpacked[:, :, 1:3].reshape(seq_rows, heads_here * 2 * HEAD_DIM)
    start_row = patch * seq_rows
    kv_all = lax.dynamic_update_slice(stale_full, fresh_kv, (start_row, jnp.zeros((), jnp.int32)))
    kv_heads = kv_all.reshape(image_rows, heads_here, 2, HEAD_DIM)
    keys_all = kv_heads[:, :, 0]
    values_all = kv_heads[:, :, 1]
    block_rows = math.gcd(seq_rows, 512)
    query_blocks = queries.reshape(seq_rows // block_rows, block_rows, heads_here, HEAD_DIM)
    inverse = HEAD_DIM ** (-0.5)

    def one_block(query_block):
        scores = (
            jnp.einsum("qhe,khe->hqk", query_block, keys_all, preferred_element_type=jnp.float32)
            * inverse
        )
        weights = jnp.exp(scores - jnp.max(scores, axis=2, keepdims=True))
        probability = (weights / jnp.sum(weights, axis=2, keepdims=True)).astype(jnp.bfloat16)
        return jnp.einsum(
            "hqk,khe->qhe", probability, values_all, preferred_element_type=jnp.float32
        ).astype(jnp.bfloat16)

    blocks_out = lax.map(one_block, query_blocks)
    return blocks_out.reshape(seq_rows, heads_here * HEAD_DIM)


def finish(finished, time_mod, final_table, final_weight):
    shift_row = final_table[0] + time_mod[0]
    scale_row = final_table[1] + time_mod[1]
    exit_normed = (layer_norm(finished) * (1.0 + scale_row) + shift_row).astype(jnp.bfloat16)
    return jnp.dot(exit_normed, final_weight, preferred_element_type=jnp.float32).astype(jnp.bfloat16)


def spread_exits(exits, segment_count):
    by_column = jnp.transpose(exits, (2, 0, 1))
    received = lax.all_to_all(by_column, "segment", 0, 0, tiled=True)
    last = received[segment_count - 2 :]
    return jnp.transpose(last, (1, 0, 2))[..., None]


def body(
    arriving,
    entering,
    section_start,
    timestep,
    qkv_weight,
    out_weight,
    stale_kv,
    layer_table,
    time_proj,
    final_table,
    final_weight,
):
    segment_index = lax.axis_index("segment")
    segment_count = lax.axis_size("segment")
    groups = lax.axis_size("bx") * lax.axis_size("by")
    heads = groups * 2
    section = segment_index // 2
    lane = segment_index % 2
    sections = segment_count // 2
    time_mod = time_vector(timestep, time_proj)
    table_row = lax.dynamic_index_in_dim(layer_table, section_start[section], 0, keepdims=False)
    modulation = table_row.astype(jnp.float32) + time_mod
    own_parts = (qkv_weight[0], stale_kv[0])
    partner_parts = swapped(own_parts, "segment", 0)
    first_parts = [
        jnp.where(lane == 0, mine, other) for mine, other in zip(own_parts, partner_parts)
    ]
    second_parts = [
        jnp.where(lane == 0, other, mine) for mine, other in zip(own_parts, partner_parts)
    ]
    qkv_local = jnp.concatenate([first_parts[0], second_parts[0]], axis=0)
    stale_full = jnp.concatenate([first_parts[1], second_parts[1]], axis=0)
    out_head = head_rows(out_weight[0], heads)
    holding = arriving[0]
    exit_list = []
    for tick_index in range(TICKS):
        stream_id = jnp.where(
            section >= tick_index,
            2 * (section - tick_index) + lane,
            2 * (sections + tick_index - 1 - section) + lane,
        )
        patch = stream_id % PATCHES
        if tick_index == 0:
            everyone = gathered_tokens(holding, groups)
            normed_all = (layer_norm(everyone) * (1.0 + modulation[1]) + modulation[0]).astype(
                jnp.bfloat16
            )
        else:
            normed = (layer_norm(holding) * (1.0 + modulation[1]) + modulation[0]).astype(
                jnp.bfloat16
            )
            normed_all = gathered_tokens(normed, groups)
        by_head = jnp.dot(normed_all, qkv_local, preferred_element_type=jnp.float32).astype(
            jnp.bfloat16
        )
        head_out = attend(by_head, stale_full, patch)
        partial = jnp.dot(head_out, out_head, preferred_element_type=jnp.float32)
        attended = scattered_sum(partial, groups)
        finished = (holding.astype(jnp.float32) + modulation[2] * attended).astype(jnp.bfloat16)
        exit_list.append(finish(finished, time_mod, final_table, final_weight))
        passed = shifted(finished, "segment", 2)
        incoming = lax.dynamic_index_in_dim(entering[tick_index], lane, 0, keepdims=False)
        holding = jnp.where(segment_index < 2, incoming, passed)
    return (holding[None], spread_exits(jnp.stack(exit_list), segment_count))


def solution(mesh):
    blk_size = mesh.shape["blk"]
    split = Mesh(
        mesh.devices.reshape(mesh.shape["segment"], blk_size // 4, 2, 2),
        ("segment",) + BLK,
    )
    in_specs = (
        P("segment", BLK, None),
        P(None, None, BLK, None),
        P(),
        P(),
        P("segment", None, BLK),
        P("segment", BLK, None),
        P("segment", None, BLK),
        P(),
        P(),
        P(),
        P(),
    )
    out_specs = (P("segment", BLK, None), P(None, None, BLK, "segment"))
    return jax.shard_map(body, mesh=split, in_specs=in_specs, out_specs=out_specs, check_vma=False)
```

```python
import jax
import jax.numpy as jnp
from jax import lax
from jax.sharding import Mesh
from jax.sharding import PartitionSpec as P

D = 1152
FREQ = 256
TICKS = 2
PATCHES = 4
HEAD_DIM = 72

BLK = ("bx", "by", "bc")
SAME_CORE = ("bx", "by")
CORE = "bc"


epsilon = 1e-06


def swapped(value, axis, apart):
    mask = 2**apart
    pairs = [(source, source ^ mask) for source in range(lax.axis_size(axis))]
    return lax.ppermute(value, axis, pairs)


def core_swapped(value):
    return lax.ppermute(value, CORE, [(0, 1), (1, 0)])


def shifted(array, axis, by):
    peers = lax.axis_size(axis)
    pairs = [(i, i + by) for i in range(peers) if 0 <= i + by < peers]
    return lax.ppermute(array, axis, pairs)


def gathered_tokens(value, groups):
    copies = jnp.broadcast_to(value[None], (groups,) + value.shape)
    same_core = lax.all_to_all(copies, SAME_CORE, 0, 0, tiled=True)
    return same_core.reshape((groups * value.shape[0],) + value.shape[1:])


def scattered_sum(partial, groups):
    chunks = partial.astype(jnp.bfloat16).reshape(groups, -1, partial.shape[1])
    received = lax.all_to_all(chunks, SAME_CORE, 0, 0, tiled=True)
    return jnp.sum(received.astype(jnp.float32), axis=0)


def head_rows(out_rows, heads):
    segment_index = lax.axis_index("segment")
    lane = segment_index % 2
    per_half = heads // 2
    segments = lax.axis_size("segment")
    moved = []
    for flip in range(2):
        pairs = []
        for segment in range(segments):
            for j in range(heads):
                source_lane = segment % 2
                target_lane = (j % 2) ^ flip
                target = (segment - source_lane + target_lane) * heads + source_lane * per_half + j // 2
                pairs.append((segment * heads + j, target))
        moved.append(lax.ppermute(out_rows, ("segment",) + BLK, pairs))
    first = jnp.where(lane == 0, moved[0], moved[1])
    second = jnp.where(lane == 0, moved[1], moved[0])
    return jnp.concatenate([first, second], axis=0)


def time_vector(timestep, time_proj):
    half_freq = FREQ // 2
    steps_k = jnp.arange(half_freq, dtype=jnp.float32)
    frequency = jnp.exp(-jnp.log(10000.0) * steps_k / half_freq)
    angles = timestep[0].astype(jnp.float32) * frequency
    embedding = jnp.concatenate([jnp.cos(angles), jnp.sin(angles)])
    time_feature = jax.nn.silu(embedding).astype(jnp.bfloat16)
    return jnp.dot(time_feature[None, :], time_proj, preferred_element_type=jnp.float32).reshape(
        3, D
    )


def layer_norm(values):
    widened = values.astype(jnp.float32)
    average = jnp.mean(widened, axis=-1, keepdims=True)
    centred = widened - average
    variance = jnp.mean(centred * centred, axis=-1, keepdims=True)
    return centred * lax.rsqrt(variance + epsilon)


def attend(queries, fresh_kv, stale_kv, patch):
    start_row = patch * fresh_kv.shape[0]
    zero = jnp.zeros((), jnp.int32)
    kv_all = lax.dynamic_update_slice(stale_kv, fresh_kv, (start_row, zero, zero, zero))
    keys_all = kv_all[:, :, 0]
    values_all = kv_all[:, :, 1]
    inverse = HEAD_DIM ** (-0.5)
    scores = (
        jnp.einsum("qhe,khe->hqk", queries, keys_all, preferred_element_type=jnp.float32) * inverse
    )
    weights = jnp.exp(scores - jnp.max(scores, axis=2, keepdims=True))
    probability = (weights / jnp.sum(weights, axis=2, keepdims=True)).astype(jnp.bfloat16)
    return jnp.einsum(
        "hqk,khe->qhe", probability, values_all, preferred_element_type=jnp.float32
    ).astype(jnp.bfloat16)


def finish(finished, time_mod, final_table, final_weight):
    shift_row = final_table[0] + time_mod[0]
    scale_row = final_table[1] + time_mod[1]
    exit_normed = (layer_norm(finished) * (1.0 + scale_row) + shift_row).astype(jnp.bfloat16)
    return jnp.dot(exit_normed, final_weight, preferred_element_type=jnp.float32).astype(jnp.bfloat16)


def spread_exits(exits, segment_count):
    by_column = jnp.transpose(exits, (2, 0, 1))
    received = lax.all_to_all(by_column, "segment", 0, 0, tiled=True)
    last = received[segment_count - 2 :]
    return jnp.transpose(last, (1, 0, 2))[..., None]


def body(
    arriving,
    entering,
    section_start,
    timestep,
    qkv_weight,
    out_weight,
    stale_kv,
    layer_table,
    time_proj,
    final_table,
    final_weight,
):
    segment_index = lax.axis_index("segment")
    segment_count = lax.axis_size("segment")
    groups = lax.axis_size("bx") * lax.axis_size("by")
    heads = groups * 2
    section = segment_index // 2
    lane = segment_index % 2
    sections = segment_count // 2
    time_mod = time_vector(timestep, time_proj)
    table_row = lax.dynamic_index_in_dim(layer_table, section_start[section], 0, keepdims=False)
    modulation = table_row.astype(jnp.float32) + time_mod
    own_parts = (qkv_weight[0], stale_kv[0])
    partner_parts = swapped(own_parts, "segment", 0)
    first_parts = [
        jnp.where(lane == 0, mine, other) for mine, other in zip(own_parts, partner_parts)
    ]
    second_parts = [
        jnp.where(lane == 0, other, mine) for mine, other in zip(own_parts, partner_parts)
    ]
    qkv_local = jnp.concatenate([first_parts[0], second_parts[0]], axis=0)
    stale_full = jnp.concatenate([first_parts[1], second_parts[1]], axis=0)
    out_head = head_rows(out_weight[0], heads)
    partner_qkv, partner_stale, partner_out = core_swapped((qkv_local, stale_full, out_head))
    qkv_pair = jnp.concatenate([qkv_local, partner_qkv], axis=1)
    image_rows = stale_full.shape[0]
    stale_pair = jnp.stack([stale_full, partner_stale], axis=1).reshape(image_rows, 2, 2, HEAD_DIM)
    out_pair = jnp.concatenate([out_head, partner_out], axis=0)
    holding = arriving[0]
    exit_list = []
    for tick_index in range(TICKS):
        stream_id = jnp.where(
            section >= tick_index,
            2 * (section - tick_index) + lane,
            2 * (sections + tick_index - 1 - section) + lane,
        )
        patch = stream_id % PATCHES
        normed = (layer_norm(holding) * (1.0 + modulation[1]) + modulation[0]).astype(jnp.bfloat16)
        tokens = gathered_tokens(normed, groups)
        projected = jnp.dot(tokens, qkv_pair, preferred_element_type=jnp.float32).astype(jnp.bfloat16)
        projected = projected.reshape(tokens.shape[0], 2, 3, HEAD_DIM)
        own_kv = projected[:, :, 1:3]
        partner_kv = core_swapped(own_kv)[:, ::-1]
        fresh_kv = jnp.concatenate([own_kv, partner_kv], axis=0)
        head_out = attend(projected[:, :, 0], fresh_kv, stale_pair, patch)
        partial = jnp.dot(
            head_out.reshape(tokens.shape[0], 2 * HEAD_DIM), out_pair, preferred_element_type=jnp.float32
        )
        attended = scattered_sum(partial, groups)
        finished = (holding.astype(jnp.float32) + modulation[2] * attended).astype(jnp.bfloat16)
        exit_list.append(finish(finished, time_mod, final_table, final_weight))
        passed = shifted(finished, "segment", 2)
        incoming = lax.dynamic_index_in_dim(entering[tick_index], lane, 0, keepdims=False)
        holding = jnp.where(segment_index < 2, incoming, passed)
    return (holding[None], spread_exits(jnp.stack(exit_list), segment_count))


def solution(mesh):
    blk_size = mesh.shape["blk"]
    split = Mesh(
        mesh.devices.reshape(mesh.shape["segment"], blk_size // 4, 2, 2),
        ("segment",) + BLK,
    )
    in_specs = (
        P("segment", BLK, None),
        P(None, None, BLK, None),
        P(),
        P(),
        P("segment", None, BLK),
        P("segment", BLK, None),
        P("segment", None, BLK),
        P(),
        P(),
        P(),
        P(),
    )
    out_specs = (P("segment", BLK, None), P(None, None, BLK, "segment"))
    return jax.shard_map(body, mesh=split, in_specs=in_specs, out_specs=out_specs, check_vma=False)
```

```python
import math

import jax
import jax.numpy as jnp
from jax import lax
from jax.sharding import Mesh
from jax.sharding import PartitionSpec as P

D = 1152
FREQ = 256
TICKS = 2
PATCHES = 4
HEAD_DIM = 72

BLK = ("bx", "by", "bc")
SAME_CORE = ("bx", "by")
CORE = "bc"


epsilon = 1e-06


def swapped(value, axis, apart):
    mask = 2**apart
    pairs = [(source, source ^ mask) for source in range(lax.axis_size(axis))]
    return lax.ppermute(value, axis, pairs)


def core_swapped(value):
    return lax.ppermute(value, CORE, [(0, 1), (1, 0)])


def shifted(array, axis, by):
    peers = lax.axis_size(axis)
    pairs = [(i, i + by) for i in range(peers) if 0 <= i + by < peers]
    return lax.ppermute(array, axis, pairs)


def gathered_tokens(value, groups):
    copies = jnp.broadcast_to(value[None], (groups,) + value.shape)
    same_core = lax.all_to_all(copies, SAME_CORE, 0, 0, tiled=True)
    other_core = core_swapped(same_core)
    core = lax.axis_index(CORE)
    first = jnp.where(core == 0, same_core, other_core)
    second = jnp.where(core == 0, other_core, same_core)
    both = jnp.stack([first, second], axis=1)
    return both.reshape((groups * 2 * value.shape[0],) + value.shape[1:])


def scattered_sum(partial, groups):
    rows = partial.shape[0] // (groups * 2)
    parts = partial.reshape(groups, 2, rows, partial.shape[1])
    core = lax.axis_index(CORE)
    mine = jnp.where(core == 0, parts[:, 0], parts[:, 1])
    theirs = jnp.where(core == 0, parts[:, 1], parts[:, 0])
    summed = (mine + core_swapped(theirs.astype(jnp.bfloat16)).astype(jnp.float32)).astype(jnp.bfloat16)
    received = lax.all_to_all(summed, SAME_CORE, 0, 0, tiled=True)
    return jnp.sum(received.astype(jnp.float32), axis=0)


def head_rows(out_rows, heads):
    segment_index = lax.axis_index("segment")
    lane = segment_index % 2
    per_half = heads // 2
    segments = lax.axis_size("segment")
    moved = []
    for flip in range(2):
        pairs = []
        for segment in range(segments):
            for j in range(heads):
                source_lane = segment % 2
                target_lane = (j % 2) ^ flip
                target = (segment - source_lane + target_lane) * heads + source_lane * per_half + j // 2
                pairs.append((segment * heads + j, target))
        moved.append(lax.ppermute(out_rows, ("segment",) + BLK, pairs))
    first = jnp.where(lane == 0, moved[0], moved[1])
    second = jnp.where(lane == 0, moved[1], moved[0])
    return jnp.concatenate([first, second], axis=0)


def time_vector(timestep, time_proj):
    half_freq = FREQ // 2
    steps_k = jnp.arange(half_freq, dtype=jnp.float32)
    frequency = jnp.exp(-jnp.log(10000.0) * steps_k / half_freq)
    angles = timestep[0].astype(jnp.float32) * frequency
    embedding = jnp.concatenate([jnp.cos(angles), jnp.sin(angles)])
    time_feature = jax.nn.silu(embedding).astype(jnp.bfloat16)
    return jnp.dot(time_feature[None, :], time_proj, preferred_element_type=jnp.float32).reshape(
        3, D
    )


def layer_norm(values):
    widened = values.astype(jnp.float32)
    average = jnp.mean(widened, axis=-1, keepdims=True)
    centred = widened - average
    variance = jnp.mean(centred * centred, axis=-1, keepdims=True)
    return centred * lax.rsqrt(variance + epsilon)


def attend(by_head, stale_full, patch):
    seq_rows = by_head.shape[0]
    image_rows = stale_full.shape[0]
    heads_here = by_head.shape[1] // (3 * HEAD_DIM)
    unpacked = by_head.reshape(seq_rows, heads_here, 3, HEAD_DIM)
    queries = unpacked[:, :, 0]
    fresh_kv = unpacked[:, :, 1:3].reshape(seq_rows, heads_here * 2 * HEAD_DIM)
    start_row = patch * seq_rows
    kv_all = lax.dynamic_update_slice(stale_full, fresh_kv, (start_row, jnp.zeros((), jnp.int32)))
    kv_heads = kv_all.reshape(image_rows, heads_here, 2, HEAD_DIM)
    keys_all = kv_heads[:, :, 0]
    values_all = kv_heads[:, :, 1]
    block_rows = math.gcd(seq_rows, 512)
    query_blocks = queries.reshape(seq_rows // block_rows, block_rows, heads_here, HEAD_DIM)
    inverse = HEAD_DIM ** (-0.5)

    def one_block(query_block):
        scores = (
            jnp.einsum("qhe,khe->hqk", query_block, keys_all, preferred_element_type=jnp.float32)
            * inverse
        )
        weights = jnp.exp(scores - jnp.max(scores, axis=2, keepdims=True))
        probability = (weights / jnp.sum(weights, axis=2, keepdims=True)).astype(jnp.bfloat16)
        return jnp.einsum(
            "hqk,khe->qhe", probability, values_all, preferred_element_type=jnp.float32
        ).astype(jnp.bfloat16)

    blocks_out = lax.map(one_block, query_blocks)
    return blocks_out.reshape(seq_rows, heads_here * HEAD_DIM)


def finish(finished, time_mod, final_table, final_weight):
    shift_row = final_table[0] + time_mod[0]
    scale_row = final_table[1] + time_mod[1]
    exit_normed = (layer_norm(finished) * (1.0 + scale_row) + shift_row).astype(jnp.bfloat16)
    return jnp.dot(exit_normed, final_weight, preferred_element_type=jnp.float32).astype(jnp.bfloat16)


def spread_exits(exits, segment_count):
    by_column = jnp.transpose(exits, (2, 0, 1))
    received = lax.all_to_all(by_column, "segment", 0, 0, tiled=True)
    last = received[segment_count - 2 :]
    return jnp.transpose(last, (1, 0, 2))[..., None]


def body(
    arriving,
    entering,
    section_start,
    timestep,
    qkv_weight,
    out_weight,
    stale_kv,
    layer_table,
    time_proj,
    final_table,
    final_weight,
):
    segment_index = lax.axis_index("segment")
    segment_count = lax.axis_size("segment")
    groups = lax.axis_size("bx") * lax.axis_size("by")
    heads = groups * 2
    section = segment_index // 2
    lane = segment_index % 2
    sections = segment_count // 2
    time_mod = time_vector(timestep, time_proj)
    table_row = lax.dynamic_index_in_dim(layer_table, section_start[section], 0, keepdims=False)
    modulation = table_row.astype(jnp.float32) + time_mod
    own_parts = (qkv_weight[0], stale_kv[0])
    partner_parts = swapped(own_parts, "segment", 0)
    first_parts = [
        jnp.where(lane == 0, mine, other) for mine, other in zip(own_parts, partner_parts)
    ]
    second_parts = [
        jnp.where(lane == 0, other, mine) for mine, other in zip(own_parts, partner_parts)
    ]
    qkv_local = jnp.concatenate([first_parts[0], second_parts[0]], axis=0)
    stale_full = jnp.concatenate([first_parts[1], second_parts[1]], axis=0)
    out_head = head_rows(out_weight[0], heads)
    holding = arriving[0]
    exit_list = []
    for tick_index in range(TICKS):
        stream_id = jnp.where(
            section >= tick_index,
            2 * (section - tick_index) + lane,
            2 * (sections + tick_index - 1 - section) + lane,
        )
        patch = stream_id % PATCHES
        normed = (layer_norm(holding) * (1.0 + modulation[1]) + modulation[0]).astype(jnp.bfloat16)
        by_head = jnp.dot(
            gathered_tokens(normed, groups),
            qkv_local,
            preferred_element_type=jnp.float32,
        ).astype(jnp.bfloat16)
        head_out = attend(by_head, stale_full, patch)
        partial = jnp.dot(head_out, out_head, preferred_element_type=jnp.float32)
        attended = scattered_sum(partial, groups)
        finished = (holding.astype(jnp.float32) + modulation[2] * attended).astype(jnp.bfloat16)
        exit_list.append(finish(finished, time_mod, final_table, final_weight))
        passed = shifted(finished, "segment", 2)
        incoming = lax.dynamic_index_in_dim(entering[tick_index], lane, 0, keepdims=False)
        holding = jnp.where(segment_index < 2, incoming, passed)
    return (holding[None], spread_exits(jnp.stack(exit_list), segment_count))


def solution(mesh):
    blk_size = mesh.shape["blk"]
    split = Mesh(
        mesh.devices.reshape(mesh.shape["segment"], blk_size // 4, 2, 2),
        ("segment",) + BLK,
    )
    in_specs = (
        P("segment", BLK, None),
        P(None, None, BLK, None),
        P(),
        P(),
        P("segment", None, BLK),
        P("segment", BLK, None),
        P("segment", None, BLK),
        P(),
        P(),
        P(),
        P(),
    )
    out_specs = (P("segment", BLK, None), P(None, None, BLK, "segment"))
    return jax.shard_map(body, mesh=split, in_specs=in_specs, out_specs=out_specs, check_vma=False)
```

```python
import math

import jax
import jax.numpy as jnp
from jax import lax
from jax.sharding import Mesh
from jax.sharding import PartitionSpec as P

D = 1152
FREQ = 256
TICKS = 2
PATCHES = 4
HEAD_DIM = 72

BLK = ("bx", "by", "bc")
SAME_CORE = ("bx", "by")
CORE = "bc"


epsilon = 1e-06


def swapped(value, axis, apart):
    mask = 2**apart
    pairs = [(source, source ^ mask) for source in range(lax.axis_size(axis))]
    return lax.ppermute(value, axis, pairs)


def core_swapped(value):
    return lax.ppermute(value, CORE, [(0, 1), (1, 0)])


def shifted(array, axis, by):
    peers = lax.axis_size(axis)
    pairs = [(i, i + by) for i in range(peers) if 0 <= i + by < peers]
    return lax.ppermute(array, axis, pairs)


def gathered_tokens(value, groups):
    copies = jnp.broadcast_to(value[None], (groups,) + value.shape)
    same_core = lax.all_to_all(copies, SAME_CORE, 0, 0, tiled=True)
    other_core = core_swapped(same_core)
    core = lax.axis_index(CORE)
    first = jnp.where(core == 0, same_core, other_core)
    second = jnp.where(core == 0, other_core, same_core)
    both = jnp.stack([first, second], axis=1)
    return both.reshape((groups * 2 * value.shape[0],) + value.shape[1:])


def scattered_sum(partial, groups):
    rows = partial.shape[0] // (groups * 2)
    parts = partial.reshape(groups, 2, rows, partial.shape[1])
    core = lax.axis_index(CORE)
    mine = jnp.where(core == 0, parts[:, 0], parts[:, 1])
    theirs = jnp.where(core == 0, parts[:, 1], parts[:, 0])
    summed = (mine + core_swapped(theirs.astype(jnp.bfloat16)).astype(jnp.float32)).astype(jnp.bfloat16)
    received = lax.all_to_all(summed, SAME_CORE, 0, 0, tiled=True)
    return jnp.sum(received.astype(jnp.float32), axis=0)


def head_rows(out_rows, heads):
    segment_index = lax.axis_index("segment")
    lane = segment_index % 2
    per_half = heads // 2
    segments = lax.axis_size("segment")
    moved = []
    for flip in range(2):
        pairs = []
        for segment in range(segments):
            for j in range(heads):
                source_lane = segment % 2
                target_lane = (j % 2) ^ flip
                target = (segment - source_lane + target_lane) * heads + source_lane * per_half + j // 2
                pairs.append((segment * heads + j, target))
        moved.append(lax.ppermute(out_rows, ("segment",) + BLK, pairs))
    first = jnp.where(lane == 0, moved[0], moved[1])
    second = jnp.where(lane == 0, moved[1], moved[0])
    return jnp.concatenate([first, second], axis=0)


def time_vector(timestep, time_proj):
    half_freq = FREQ // 2
    steps_k = jnp.arange(half_freq, dtype=jnp.float32)
    frequency = jnp.exp(-jnp.log(10000.0) * steps_k / half_freq)
    angles = timestep[0].astype(jnp.float32) * frequency
    embedding = jnp.concatenate([jnp.cos(angles), jnp.sin(angles)])
    time_feature = jax.nn.silu(embedding).astype(jnp.bfloat16)
    return jnp.dot(time_feature[None, :], time_proj, preferred_element_type=jnp.float32).reshape(
        3, D
    )


def layer_norm(values):
    widened = values.astype(jnp.float32)
    average = jnp.mean(widened, axis=-1, keepdims=True)
    centred = widened - average
    variance = jnp.mean(centred * centred, axis=-1, keepdims=True)
    return centred * lax.rsqrt(variance + epsilon)


def attend(by_head, stale_full, patch):
    seq_rows = by_head.shape[0]
    image_rows = stale_full.shape[0]
    heads_here = by_head.shape[1] // (3 * HEAD_DIM)
    unpacked = by_head.reshape(seq_rows, heads_here, 3, HEAD_DIM)
    queries = unpacked[:, :, 0]
    fresh_kv = unpacked[:, :, 1:3].reshape(seq_rows, heads_here * 2 * HEAD_DIM)
    start_row = patch * seq_rows
    kv_all = lax.dynamic_update_slice(stale_full, fresh_kv, (start_row, jnp.zeros((), jnp.int32)))
    kv_heads = kv_all.reshape(image_rows, heads_here, 2, HEAD_DIM)
    keys_all = kv_heads[:, :, 0]
    values_all = kv_heads[:, :, 1]
    block_rows = math.gcd(seq_rows, 512)
    query_blocks = queries.reshape(seq_rows // block_rows, block_rows, heads_here, HEAD_DIM)
    inverse = HEAD_DIM ** (-0.5)

    def one_block(query_block):
        scores = (
            jnp.einsum("qhe,khe->hqk", query_block, keys_all, preferred_element_type=jnp.float32)
            * inverse
        )
        weights = jnp.exp(scores - jnp.max(scores, axis=2, keepdims=True))
        probability = (weights / jnp.sum(weights, axis=2, keepdims=True)).astype(jnp.bfloat16)
        return jnp.einsum(
            "hqk,khe->qhe", probability, values_all, preferred_element_type=jnp.float32
        ).astype(jnp.bfloat16)

    blocks_out = lax.map(one_block, query_blocks)
    return blocks_out.reshape(seq_rows, heads_here * HEAD_DIM)


def finish(finished, time_mod, final_table, final_weight):
    shift_row = final_table[0] + time_mod[0]
    scale_row = final_table[1] + time_mod[1]
    exit_normed = (layer_norm(finished) * (1.0 + scale_row) + shift_row).astype(jnp.bfloat16)
    return jnp.dot(exit_normed, final_weight, preferred_element_type=jnp.float32).astype(jnp.bfloat16)


def spread_exits(exits, segment_count):
    by_column = jnp.transpose(exits, (2, 0, 1))
    received = lax.all_to_all(by_column, "segment", 0, 0, tiled=True)
    last = received[segment_count - 2 :]
    return jnp.transpose(last, (1, 0, 2))[..., None]


def body(
    arriving,
    entering,
    section_start,
    timestep,
    qkv_weight,
    out_weight,
    stale_kv,
    layer_table,
    time_proj,
    final_table,
    final_weight,
):
    segment_index = lax.axis_index("segment")
    segment_count = lax.axis_size("segment")
    groups = lax.axis_size("bx") * lax.axis_size("by")
    heads = groups * 2
    section = segment_index // 2
    lane = segment_index % 2
    sections = segment_count // 2
    time_mod = time_vector(timestep, time_proj)
    first_layer = jnp.sum(jnp.where(jnp.arange(sections) == section, section_start, 0))
    layer_rows = jnp.arange(layer_table.shape[0])[:, None, None] == first_layer
    table_row = jnp.sum(jnp.where(layer_rows, layer_table.astype(jnp.float32), 0.0), axis=0)
    modulation = table_row + time_mod
    own_parts = (qkv_weight[0], stale_kv[0])
    partner_parts = swapped(own_parts, "segment", 0)
    first_parts = [
        jnp.where(lane == 0, mine, other) for mine, other in zip(own_parts, partner_parts)
    ]
    second_parts = [
        jnp.where(lane == 0, other, mine) for mine, other in zip(own_parts, partner_parts)
    ]
    qkv_local = jnp.concatenate([first_parts[0], second_parts[0]], axis=0)
    stale_full = jnp.concatenate([first_parts[1], second_parts[1]], axis=0)
    out_head = head_rows(out_weight[0], heads)
    holding = arriving[0]
    exit_list = []
    for tick_index in range(TICKS):
        stream_id = jnp.where(
            section >= tick_index,
            2 * (section - tick_index) + lane,
            2 * (sections + tick_index - 1 - section) + lane,
        )
        patch = stream_id % PATCHES
        normed = (layer_norm(holding) * (1.0 + modulation[1]) + modulation[0]).astype(jnp.bfloat16)
        by_head = jnp.dot(
            gathered_tokens(normed, groups),
            qkv_local,
            preferred_element_type=jnp.float32,
        ).astype(jnp.bfloat16)
        head_out = attend(by_head, stale_full, patch)
        partial = jnp.dot(head_out, out_head, preferred_element_type=jnp.float32)
        attended = scattered_sum(partial, groups)
        finished = (holding.astype(jnp.float32) + modulation[2] * attended).astype(jnp.bfloat16)
        exit_list.append(finish(finished, time_mod, final_table, final_weight))
        passed = shifted(finished, "segment", 2)
        incoming = lax.dynamic_index_in_dim(entering[tick_index], lane, 0, keepdims=False)
        holding = jnp.where(segment_index < 2, incoming, passed)
    return (holding[None], spread_exits(jnp.stack(exit_list), segment_count))


def solution(mesh):
    blk_size = mesh.shape["blk"]
    split = Mesh(
        mesh.devices.reshape(mesh.shape["segment"], blk_size // 4, 2, 2),
        ("segment",) + BLK,
    )
    in_specs = (
        P("segment", BLK, None),
        P(None, None, BLK, None),
        P(),
        P(),
        P("segment", None, BLK),
        P("segment", BLK, None),
        P("segment", None, BLK),
        P(),
        P(),
        P(),
        P(),
    )
    out_specs = (P("segment", BLK, None), P(None, None, BLK, "segment"))
    return jax.shard_map(body, mesh=split, in_specs=in_specs, out_specs=out_specs, check_vma=False)
```

```python
import math

import jax
import jax.numpy as jnp
from jax import lax
from jax.sharding import Mesh
from jax.sharding import PartitionSpec as P

D = 1152
FREQ = 256
TICKS = 2
PATCHES = 4
HEAD_DIM = 72

BLK = ("bx", "by", "bc")
SAME_CORE = ("bx", "by")
CORE = "bc"


epsilon = 1e-06


def swapped(value, axis, apart):
    mask = 2**apart
    pairs = [(source, source ^ mask) for source in range(lax.axis_size(axis))]
    return lax.ppermute(value, axis, pairs)


def core_swapped(value):
    return lax.ppermute(value, CORE, [(0, 1), (1, 0)])


def shifted(array, axis, by):
    peers = lax.axis_size(axis)
    pairs = [(i, i + by) for i in range(peers) if 0 <= i + by < peers]
    return lax.ppermute(array, axis, pairs)


def gathered_tokens(value, groups):
    copies = jnp.broadcast_to(value[None], (groups,) + value.shape)
    same_core = lax.all_to_all(copies, SAME_CORE, 0, 0, tiled=True)
    both = jnp.stack([same_core, core_swapped(same_core)])
    return both.reshape((2 * groups * value.shape[0],) + value.shape[1:])


def scattered_sum(partial, groups):
    parts = partial.reshape(2, groups, partial.shape[0] // (2 * groups), partial.shape[1])
    theirs = core_swapped(parts[1].astype(jnp.bfloat16)).astype(jnp.float32)
    summed = (parts[0] + theirs).astype(jnp.bfloat16)
    received = lax.all_to_all(summed, SAME_CORE, 0, 0, tiled=True)
    return jnp.sum(received.astype(jnp.float32), axis=0)


def head_rows(out_rows, heads):
    segment_index = lax.axis_index("segment")
    lane = segment_index % 2
    per_half = heads // 2
    segments = lax.axis_size("segment")
    moved = []
    for flip in range(2):
        pairs = []
        for segment in range(segments):
            for j in range(heads):
                source_lane = segment % 2
                target_lane = (j % 2) ^ flip
                target = (segment - source_lane + target_lane) * heads + source_lane * per_half + j // 2
                pairs.append((segment * heads + j, target))
        moved.append(lax.ppermute(out_rows, ("segment",) + BLK, pairs))
    first = jnp.where(lane == 0, moved[0], moved[1])
    second = jnp.where(lane == 0, moved[1], moved[0])
    return jnp.concatenate([first, second], axis=0)


def time_vector(timestep, time_proj):
    half_freq = FREQ // 2
    steps_k = jnp.arange(half_freq, dtype=jnp.float32)
    frequency = jnp.exp(-jnp.log(10000.0) * steps_k / half_freq)
    angles = timestep[0].astype(jnp.float32) * frequency
    embedding = jnp.concatenate([jnp.cos(angles), jnp.sin(angles)])
    time_feature = jax.nn.silu(embedding).astype(jnp.bfloat16)
    return jnp.dot(time_feature[None, :], time_proj, preferred_element_type=jnp.float32).reshape(
        3, D
    )


def layer_norm(values):
    widened = values.astype(jnp.float32)
    average = jnp.mean(widened, axis=-1, keepdims=True)
    centred = widened - average
    variance = jnp.mean(centred * centred, axis=-1, keepdims=True)
    return centred * lax.rsqrt(variance + epsilon)


def attend(by_head, stale_full, patch):
    seq_rows = by_head.shape[0]
    image_rows = stale_full.shape[0]
    heads_here = by_head.shape[1] // (3 * HEAD_DIM)
    unpacked = by_head.reshape(seq_rows, heads_here, 3, HEAD_DIM)
    queries = unpacked[:, :, 0]
    fresh_kv = unpacked[:, :, 1:3].reshape(seq_rows, heads_here * 2 * HEAD_DIM)
    start_row = patch * seq_rows
    kv_all = lax.dynamic_update_slice(stale_full, fresh_kv, (start_row, jnp.zeros((), jnp.int32)))
    kv_heads = kv_all.reshape(image_rows, heads_here, 2, HEAD_DIM)
    keys_all = kv_heads[:, :, 0]
    values_all = kv_heads[:, :, 1]
    block_rows = math.gcd(seq_rows, 512)
    query_blocks = queries.reshape(seq_rows // block_rows, block_rows, heads_here, HEAD_DIM)
    inverse = HEAD_DIM ** (-0.5)

    def one_block(query_block):
        scores = (
            jnp.einsum("qhe,khe->hqk", query_block, keys_all, preferred_element_type=jnp.float32)
            * inverse
        )
        weights = jnp.exp(scores - jnp.max(scores, axis=2, keepdims=True))
        probability = (weights / jnp.sum(weights, axis=2, keepdims=True)).astype(jnp.bfloat16)
        return jnp.einsum(
            "hqk,khe->qhe", probability, values_all, preferred_element_type=jnp.float32
        ).astype(jnp.bfloat16)

    blocks_out = lax.map(one_block, query_blocks)
    return blocks_out.reshape(seq_rows, heads_here * HEAD_DIM)


def finish(finished, time_mod, final_table, final_weight):
    shift_row = final_table[0] + time_mod[0]
    scale_row = final_table[1] + time_mod[1]
    exit_normed = (layer_norm(finished) * (1.0 + scale_row) + shift_row).astype(jnp.bfloat16)
    return jnp.dot(exit_normed, final_weight, preferred_element_type=jnp.float32).astype(jnp.bfloat16)


def spread_exits(exits, segment_count):
    by_column = jnp.transpose(exits, (2, 0, 1))
    received = lax.all_to_all(by_column, "segment", 0, 0, tiled=True)
    last = received[segment_count - 2 :]
    return jnp.transpose(last, (1, 0, 2))[..., None]


def body(
    arriving,
    entering,
    section_start,
    timestep,
    qkv_weight,
    out_weight,
    stale_kv,
    layer_table,
    time_proj,
    final_table,
    final_weight,
):
    segment_index = lax.axis_index("segment")
    segment_count = lax.axis_size("segment")
    groups = lax.axis_size("bx") * lax.axis_size("by")
    heads = groups * 2
    section = segment_index // 2
    lane = segment_index % 2
    sections = segment_count // 2
    time_mod = time_vector(timestep, time_proj)
    first_layer = jnp.sum(jnp.where(jnp.arange(sections) == section, section_start, 0))
    layer_rows = jnp.arange(layer_table.shape[0])[:, None, None] == first_layer
    table_row = jnp.sum(jnp.where(layer_rows, layer_table.astype(jnp.float32), 0.0), axis=0)
    modulation = table_row + time_mod
    own_parts = (qkv_weight[0], stale_kv[0])
    partner_parts = swapped(own_parts, "segment", 0)
    first_parts = [
        jnp.where(lane == 0, mine, other) for mine, other in zip(own_parts, partner_parts)
    ]
    second_parts = [
        jnp.where(lane == 0, other, mine) for mine, other in zip(own_parts, partner_parts)
    ]
    qkv_local = jnp.concatenate([first_parts[0], second_parts[0]], axis=0)
    stale_full = jnp.concatenate([first_parts[1], second_parts[1]], axis=0)
    out_head = head_rows(out_weight[0], heads)
    holding = arriving[0]
    exit_list = []
    for tick_index in range(TICKS):
        stream_id = jnp.where(
            section >= tick_index,
            2 * (section - tick_index) + lane,
            2 * (sections + tick_index - 1 - section) + lane,
        )
        patch = stream_id % PATCHES
        normed = (layer_norm(holding) * (1.0 + modulation[1]) + modulation[0]).astype(jnp.bfloat16)
        by_head = jnp.dot(
            gathered_tokens(normed, groups),
            qkv_local,
            preferred_element_type=jnp.float32,
        ).astype(jnp.bfloat16)
        head_out = attend(by_head, stale_full, patch)
        partial = jnp.dot(head_out, out_head, preferred_element_type=jnp.float32)
        attended = scattered_sum(partial, groups)
        finished = (holding.astype(jnp.float32) + modulation[2] * attended).astype(jnp.bfloat16)
        exit_list.append(finish(finished, time_mod, final_table, final_weight))
        passed = shifted(finished, "segment", 2)
        incoming = lax.dynamic_index_in_dim(entering[tick_index], lane, 0, keepdims=False)
        holding = jnp.where(segment_index < 2, incoming, passed)
    return (holding[None], spread_exits(jnp.stack(exit_list), segment_count))


def solution(mesh):
    blk_size = mesh.shape["blk"]
    split = Mesh(
        mesh.devices.reshape(mesh.shape["segment"], blk_size // 4, 2, 2),
        ("segment",) + BLK,
    )
    in_specs = (
        P("segment", BLK, None),
        P(None, None, BLK, None),
        P(),
        P(),
        P("segment", None, BLK),
        P("segment", BLK, None),
        P("segment", None, BLK),
        P(),
        P(),
        P(),
        P(),
    )
    out_specs = (P("segment", BLK, None), P(None, None, BLK, "segment"))
    return jax.shard_map(body, mesh=split, in_specs=in_specs, out_specs=out_specs, check_vma=False)
```

```python
import math

import jax
import jax.numpy as jnp
from jax import lax
from jax.sharding import Mesh
from jax.sharding import PartitionSpec as P

D = 1152
FREQ = 256
TICKS = 2
PATCHES = 4
HEAD_DIM = 72

BLK = ("bx", "by", "bc")
SAME_CORE = ("bx", "by")
CORE = "bc"


epsilon = 1e-06


def swapped(value, axis, apart):
    mask = 2**apart
    pairs = [(source, source ^ mask) for source in range(lax.axis_size(axis))]
    return lax.ppermute(value, axis, pairs)


def core_swapped(value):
    return lax.ppermute(value, CORE, [(0, 1), (1, 0)])


def shifted(array, axis, by):
    peers = lax.axis_size(axis)
    pairs = [(i, i + by) for i in range(peers) if 0 <= i + by < peers]
    return lax.ppermute(array, axis, pairs)


def gathered_tokens(value, groups):
    copies = jnp.broadcast_to(value[None], (groups,) + value.shape)
    same_core = lax.all_to_all(copies, SAME_CORE, 0, 0, tiled=True)
    both = jnp.stack([same_core, core_swapped(same_core)])
    return both.reshape((2 * groups * value.shape[0],) + value.shape[1:])


def scattered_sum(head_out, out_head, groups):
    rows = head_out.shape[0] // 2
    theirs = jnp.dot(head_out[rows:], out_head, preferred_element_type=jnp.float32)
    moved = core_swapped(theirs.astype(jnp.bfloat16)).astype(jnp.float32)
    mine = jnp.dot(head_out[:rows], out_head, preferred_element_type=jnp.float32)
    summed = (mine + moved).astype(jnp.bfloat16).reshape(groups, -1, out_head.shape[1])
    received = lax.all_to_all(summed, SAME_CORE, 0, 0, tiled=True)
    return jnp.sum(received.astype(jnp.float32), axis=0)


def head_rows(out_rows, heads):
    segment_index = lax.axis_index("segment")
    lane = segment_index % 2
    per_half = heads // 2
    segments = lax.axis_size("segment")
    moved = []
    for flip in range(2):
        pairs = []
        for segment in range(segments):
            for j in range(heads):
                source_lane = segment % 2
                target_lane = (j % 2) ^ flip
                target = (segment - source_lane + target_lane) * heads + source_lane * per_half + j // 2
                pairs.append((segment * heads + j, target))
        moved.append(lax.ppermute(out_rows, ("segment",) + BLK, pairs))
    first = jnp.where(lane == 0, moved[0], moved[1])
    second = jnp.where(lane == 0, moved[1], moved[0])
    return jnp.concatenate([first, second], axis=0)


def time_vector(timestep, time_proj):
    half_freq = FREQ // 2
    steps_k = jnp.arange(half_freq, dtype=jnp.float32)
    frequency = jnp.exp(-jnp.log(10000.0) * steps_k / half_freq)
    angles = timestep[0].astype(jnp.float32) * frequency
    embedding = jnp.concatenate([jnp.cos(angles), jnp.sin(angles)])
    time_feature = jax.nn.silu(embedding).astype(jnp.bfloat16)
    return jnp.dot(time_feature[None, :], time_proj, preferred_element_type=jnp.float32).reshape(
        3, D
    )


def layer_norm(values):
    widened = values.astype(jnp.float32)
    average = jnp.mean(widened, axis=-1, keepdims=True)
    centred = widened - average
    variance = jnp.mean(centred * centred, axis=-1, keepdims=True)
    return centred * lax.rsqrt(variance + epsilon)


def attend(by_head, stale_full, patch):
    seq_rows = by_head.shape[0]
    image_rows = stale_full.shape[0]
    heads_here = by_head.shape[1] // (3 * HEAD_DIM)
    unpacked = by_head.reshape(seq_rows, heads_here, 3, HEAD_DIM)
    queries = unpacked[:, :, 0]
    fresh_kv = unpacked[:, :, 1:3].reshape(seq_rows, heads_here * 2 * HEAD_DIM)
    start_row = patch * seq_rows
    kv_all = lax.dynamic_update_slice(stale_full, fresh_kv, (start_row, jnp.zeros((), jnp.int32)))
    kv_heads = kv_all.reshape(image_rows, heads_here, 2, HEAD_DIM)
    keys_all = kv_heads[:, :, 0]
    values_all = kv_heads[:, :, 1]
    block_rows = math.gcd(seq_rows, 512)
    query_blocks = queries.reshape(seq_rows // block_rows, block_rows, heads_here, HEAD_DIM)
    inverse = HEAD_DIM ** (-0.5)

    def one_block(query_block):
        scores = (
            jnp.einsum("qhe,khe->hqk", query_block, keys_all, preferred_element_type=jnp.float32)
            * inverse
        )
        weights = jnp.exp(scores - jnp.max(scores, axis=2, keepdims=True))
        probability = (weights / jnp.sum(weights, axis=2, keepdims=True)).astype(jnp.bfloat16)
        return jnp.einsum(
            "hqk,khe->qhe", probability, values_all, preferred_element_type=jnp.float32
        ).astype(jnp.bfloat16)

    blocks_out = lax.map(one_block, query_blocks)
    return blocks_out.reshape(seq_rows, heads_here * HEAD_DIM)


def finish(finished, time_mod, final_table, final_weight):
    shift_row = final_table[0] + time_mod[0]
    scale_row = final_table[1] + time_mod[1]
    exit_normed = (layer_norm(finished) * (1.0 + scale_row) + shift_row).astype(jnp.bfloat16)
    return jnp.dot(exit_normed, final_weight, preferred_element_type=jnp.float32).astype(jnp.bfloat16)


def spread_exits(exits, segment_count):
    by_column = jnp.transpose(exits, (2, 0, 1))
    received = lax.all_to_all(by_column, "segment", 0, 0, tiled=True)
    last = received[segment_count - 2 :]
    return jnp.transpose(last, (1, 0, 2))[..., None]


def body(
    arriving,
    entering,
    section_start,
    timestep,
    qkv_weight,
    out_weight,
    stale_kv,
    layer_table,
    time_proj,
    final_table,
    final_weight,
):
    segment_index = lax.axis_index("segment")
    segment_count = lax.axis_size("segment")
    groups = lax.axis_size("bx") * lax.axis_size("by")
    heads = groups * 2
    section = segment_index // 2
    lane = segment_index % 2
    sections = segment_count // 2
    time_mod = time_vector(timestep, time_proj)
    first_layer = jnp.sum(jnp.where(jnp.arange(sections) == section, section_start, 0))
    layer_rows = jnp.arange(layer_table.shape[0])[:, None, None] == first_layer
    table_row = jnp.sum(jnp.where(layer_rows, layer_table.astype(jnp.float32), 0.0), axis=0)
    modulation = table_row + time_mod
    own_parts = (qkv_weight[0], stale_kv[0])
    partner_parts = swapped(own_parts, "segment", 0)
    first_parts = [
        jnp.where(lane == 0, mine, other) for mine, other in zip(own_parts, partner_parts)
    ]
    second_parts = [
        jnp.where(lane == 0, other, mine) for mine, other in zip(own_parts, partner_parts)
    ]
    qkv_local = jnp.concatenate([first_parts[0], second_parts[0]], axis=0)
    stale_full = jnp.concatenate([first_parts[1], second_parts[1]], axis=0)
    out_head = head_rows(out_weight[0], heads)
    holding = arriving[0]
    exit_list = []
    for tick_index in range(TICKS):
        stream_id = jnp.where(
            section >= tick_index,
            2 * (section - tick_index) + lane,
            2 * (sections + tick_index - 1 - section) + lane,
        )
        patch = stream_id % PATCHES
        normed = (layer_norm(holding) * (1.0 + modulation[1]) + modulation[0]).astype(jnp.bfloat16)
        by_head = jnp.dot(
            gathered_tokens(normed, groups),
            qkv_local,
            preferred_element_type=jnp.float32,
        ).astype(jnp.bfloat16)
        head_out = attend(by_head, stale_full, patch)
        attended = scattered_sum(head_out, out_head, groups)
        finished = (holding.astype(jnp.float32) + modulation[2] * attended).astype(jnp.bfloat16)
        exit_list.append(finish(finished, time_mod, final_table, final_weight))
        passed = shifted(finished, "segment", 2)
        incoming = lax.dynamic_index_in_dim(entering[tick_index], lane, 0, keepdims=False)
        holding = jnp.where(segment_index < 2, incoming, passed)
    return (holding[None], spread_exits(jnp.stack(exit_list), segment_count))


def solution(mesh):
    blk_size = mesh.shape["blk"]
    split = Mesh(
        mesh.devices.reshape(mesh.shape["segment"], blk_size // 4, 2, 2),
        ("segment",) + BLK,
    )
    in_specs = (
        P("segment", BLK, None),
        P(None, None, BLK, None),
        P(),
        P(),
        P("segment", None, BLK),
        P("segment", BLK, None),
        P("segment", None, BLK),
        P(),
        P(),
        P(),
        P(),
    )
    out_specs = (P("segment", BLK, None), P(None, None, BLK, "segment"))
    return jax.shard_map(body, mesh=split, in_specs=in_specs, out_specs=out_specs, check_vma=False)
```

```python
import math

import jax
import jax.numpy as jnp
from jax import lax
from jax.sharding import Mesh
from jax.sharding import PartitionSpec as P

D = 1152
FREQ = 256
TICKS = 2
PATCHES = 4
HEAD_DIM = 72

BLK = ("bx", "by", "bc")
SAME_CORE = ("bx", "by")
CORE = "bc"


epsilon = 1e-06


def swapped(value, axis, apart):
    mask = 2**apart
    pairs = [(source, source ^ mask) for source in range(lax.axis_size(axis))]
    return lax.ppermute(value, axis, pairs)


def core_swapped(value):
    return lax.ppermute(value, CORE, [(0, 1), (1, 0)])


def shifted(array, axis, by):
    peers = lax.axis_size(axis)
    pairs = [(i, i + by) for i in range(peers) if 0 <= i + by < peers]
    return lax.ppermute(array, axis, pairs)


def gathered_tokens(value, groups):
    copies = jnp.broadcast_to(value[None], (groups,) + value.shape)
    same_core = lax.all_to_all(copies, SAME_CORE, 0, 0, tiled=True)
    both = jnp.stack([same_core, core_swapped(same_core)])
    return both.reshape((2 * groups * value.shape[0],) + value.shape[1:])


def scattered_sum(head_out, out_head, groups):
    rows = head_out.shape[0] // 2
    theirs = jnp.dot(head_out[rows:], out_head, preferred_element_type=jnp.float32)
    moved = core_swapped(theirs.astype(jnp.bfloat16)).astype(jnp.float32)
    mine = lax.optimization_barrier(
        jnp.dot(head_out[:rows], out_head, preferred_element_type=jnp.float32)
    )
    summed = (mine + moved).astype(jnp.bfloat16).reshape(groups, -1, out_head.shape[1])
    received = lax.all_to_all(summed, SAME_CORE, 0, 0, tiled=True)
    return jnp.sum(received.astype(jnp.float32), axis=0)


def head_rows(out_rows, heads):
    segment_index = lax.axis_index("segment")
    lane = segment_index % 2
    per_half = heads // 2
    segments = lax.axis_size("segment")
    moved = []
    for flip in range(2):
        pairs = []
        for segment in range(segments):
            for j in range(heads):
                source_lane = segment % 2
                target_lane = (j % 2) ^ flip
                target = (segment - source_lane + target_lane) * heads + source_lane * per_half + j // 2
                pairs.append((segment * heads + j, target))
        moved.append(lax.ppermute(out_rows, ("segment",) + BLK, pairs))
    first = jnp.where(lane == 0, moved[0], moved[1])
    second = jnp.where(lane == 0, moved[1], moved[0])
    return jnp.concatenate([first, second], axis=0)


def time_vector(timestep, time_proj):
    half_freq = FREQ // 2
    steps_k = jnp.arange(half_freq, dtype=jnp.float32)
    frequency = jnp.exp(-jnp.log(10000.0) * steps_k / half_freq)
    angles = timestep[0].astype(jnp.float32) * frequency
    embedding = jnp.concatenate([jnp.cos(angles), jnp.sin(angles)])
    time_feature = jax.nn.silu(embedding).astype(jnp.bfloat16)
    return jnp.dot(time_feature[None, :], time_proj, preferred_element_type=jnp.float32).reshape(
        3, D
    )


def layer_norm(values):
    widened = values.astype(jnp.float32)
    average = jnp.mean(widened, axis=-1, keepdims=True)
    centred = widened - average
    variance = jnp.mean(centred * centred, axis=-1, keepdims=True)
    return centred * lax.rsqrt(variance + epsilon)


def attend(by_head, stale_full, patch):
    seq_rows = by_head.shape[0]
    image_rows = stale_full.shape[0]
    heads_here = by_head.shape[1] // (3 * HEAD_DIM)
    unpacked = by_head.reshape(seq_rows, heads_here, 3, HEAD_DIM)
    queries = unpacked[:, :, 0]
    fresh_kv = unpacked[:, :, 1:3].reshape(seq_rows, heads_here * 2 * HEAD_DIM)
    start_row = patch * seq_rows
    kv_all = lax.dynamic_update_slice(stale_full, fresh_kv, (start_row, jnp.zeros((), jnp.int32)))
    kv_heads = kv_all.reshape(image_rows, heads_here, 2, HEAD_DIM)
    keys_all = kv_heads[:, :, 0]
    values_all = kv_heads[:, :, 1]
    block_rows = math.gcd(seq_rows, 512)
    query_blocks = queries.reshape(seq_rows // block_rows, block_rows, heads_here, HEAD_DIM)
    inverse = HEAD_DIM ** (-0.5)

    def one_block(query_block):
        scores = (
            jnp.einsum("qhe,khe->hqk", query_block, keys_all, preferred_element_type=jnp.float32)
            * inverse
        )
        weights = jnp.exp(scores - jnp.max(scores, axis=2, keepdims=True))
        probability = (weights / jnp.sum(weights, axis=2, keepdims=True)).astype(jnp.bfloat16)
        return jnp.einsum(
            "hqk,khe->qhe", probability, values_all, preferred_element_type=jnp.float32
        ).astype(jnp.bfloat16)

    blocks_out = lax.map(one_block, query_blocks)
    return blocks_out.reshape(seq_rows, heads_here * HEAD_DIM)


def finish(finished, time_mod, final_table, final_weight):
    shift_row = final_table[0] + time_mod[0]
    scale_row = final_table[1] + time_mod[1]
    exit_normed = (layer_norm(finished) * (1.0 + scale_row) + shift_row).astype(jnp.bfloat16)
    return jnp.einsum(
        "fc,tf->ct", final_weight, exit_normed, preferred_element_type=jnp.float32
    ).astype(jnp.bfloat16)


def spread_exits(exits, segment_count):
    received = lax.all_to_all(exits, "segment", 0, 0, tiled=True)
    last = received[segment_count - 2 :]
    return jnp.transpose(last, (1, 0, 2))[..., None]


def body(
    arriving,
    entering,
    section_start,
    timestep,
    qkv_weight,
    out_weight,
    stale_kv,
    layer_table,
    time_proj,
    final_table,
    final_weight,
):
    segment_index = lax.axis_index("segment")
    segment_count = lax.axis_size("segment")
    groups = lax.axis_size("bx") * lax.axis_size("by")
    heads = groups * 2
    section = segment_index // 2
    lane = segment_index % 2
    sections = segment_count // 2
    time_mod = time_vector(timestep, time_proj)
    first_layer = jnp.sum(jnp.where(jnp.arange(sections) == section, section_start, 0))
    layer_rows = jnp.arange(layer_table.shape[0])[:, None, None] == first_layer
    table_row = jnp.sum(jnp.where(layer_rows, layer_table.astype(jnp.float32), 0.0), axis=0)
    modulation = table_row + time_mod
    own_parts = (qkv_weight[0], stale_kv[0])
    partner_parts = swapped(own_parts, "segment", 0)
    first_parts = [
        jnp.where(lane == 0, mine, other) for mine, other in zip(own_parts, partner_parts)
    ]
    second_parts = [
        jnp.where(lane == 0, other, mine) for mine, other in zip(own_parts, partner_parts)
    ]
    qkv_local = jnp.concatenate([first_parts[0], second_parts[0]], axis=0)
    stale_full = jnp.concatenate([first_parts[1], second_parts[1]], axis=0)
    out_head = head_rows(out_weight[0], heads)
    holding = arriving[0]
    exit_list = []
    for tick_index in range(TICKS):
        stream_id = jnp.where(
            section >= tick_index,
            2 * (section - tick_index) + lane,
            2 * (sections + tick_index - 1 - section) + lane,
        )
        patch = stream_id % PATCHES
        normed = (layer_norm(holding) * (1.0 + modulation[1]) + modulation[0]).astype(jnp.bfloat16)
        by_head = jnp.dot(
            gathered_tokens(normed, groups),
            qkv_local,
            preferred_element_type=jnp.float32,
        ).astype(jnp.bfloat16)
        head_out = attend(by_head, stale_full, patch)
        attended = scattered_sum(head_out, out_head, groups)
        finished = (holding.astype(jnp.float32) + modulation[2] * attended).astype(jnp.bfloat16)
        exit_list.append(finish(finished, time_mod, final_table, final_weight))
        passed = shifted(finished, "segment", 2)
        incoming = lax.dynamic_index_in_dim(entering[tick_index], lane, 0, keepdims=False)
        holding = jnp.where(segment_index < 2, incoming, passed)
    return (holding[None], spread_exits(jnp.stack(exit_list, axis=1), segment_count))


def solution(mesh):
    blk_size = mesh.shape["blk"]
    split = Mesh(
        mesh.devices.reshape(mesh.shape["segment"], blk_size // 4, 2, 2),
        ("segment",) + BLK,
    )
    in_specs = (
        P("segment", BLK, None),
        P(None, None, BLK, None),
        P(),
        P(),
        P("segment", None, BLK),
        P("segment", BLK, None),
        P("segment", None, BLK),
        P(),
        P(),
        P(),
        P(),
    )
    out_specs = (P("segment", BLK, None), P(None, None, BLK, "segment"))
    return jax.shard_map(body, mesh=split, in_specs=in_specs, out_specs=out_specs, check_vma=False)
```

```python
import math

import jax
import jax.numpy as jnp
from jax import lax
from jax.sharding import Mesh
from jax.sharding import PartitionSpec as P

D = 1152
FREQ = 256
TICKS = 2
PATCHES = 4
HEAD_DIM = 72

BLK = ("bx", "by", "bc")
SAME_CORE = ("bx", "by")
CORE = "bc"


epsilon = 1e-06


def swapped(value, axis, apart):
    mask = 2**apart
    pairs = [(source, source ^ mask) for source in range(lax.axis_size(axis))]
    return lax.ppermute(value, axis, pairs)


def core_swapped(value):
    return lax.ppermute(value, CORE, [(0, 1), (1, 0)])


def shifted(array, axis, by):
    peers = lax.axis_size(axis)
    pairs = [(i, i + by) for i in range(peers) if 0 <= i + by < peers]
    return lax.ppermute(array, axis, pairs)


def projected_tokens(value, groups, weight):
    copies = jnp.broadcast_to(value[None], (groups,) + value.shape)
    same_core = lax.all_to_all(copies, SAME_CORE, 0, 0, tiled=True).reshape(-1, value.shape[1])
    other_core = core_swapped(same_core)
    own = lax.optimization_barrier(
        jnp.dot(same_core, weight, preferred_element_type=jnp.float32).astype(jnp.bfloat16)
    )
    other = jnp.dot(other_core, weight, preferred_element_type=jnp.float32).astype(jnp.bfloat16)
    return jnp.concatenate([own, other], axis=0)


def scattered_sum(head_out, out_head, groups):
    rows = head_out.shape[0] // 2
    theirs = jnp.dot(head_out[rows:], out_head, preferred_element_type=jnp.float32)
    moved = core_swapped(theirs.astype(jnp.bfloat16)).astype(jnp.float32)
    mine = lax.optimization_barrier(
        jnp.dot(head_out[:rows], out_head, preferred_element_type=jnp.float32)
    )
    summed = (mine + moved).astype(jnp.bfloat16).reshape(groups, -1, out_head.shape[1])
    received = lax.all_to_all(summed, SAME_CORE, 0, 0, tiled=True)
    return jnp.sum(received.astype(jnp.float32), axis=0)


def head_rows(out_rows, heads):
    segment_index = lax.axis_index("segment")
    lane = segment_index % 2
    per_half = heads // 2
    segments = lax.axis_size("segment")
    moved = []
    for flip in range(2):
        pairs = []
        for segment in range(segments):
            for j in range(heads):
                source_lane = segment % 2
                target_lane = (j % 2) ^ flip
                target = (segment - source_lane + target_lane) * heads + source_lane * per_half + j // 2
                pairs.append((segment * heads + j, target))
        moved.append(lax.ppermute(out_rows, ("segment",) + BLK, pairs))
    first = jnp.where(lane == 0, moved[0], moved[1])
    second = jnp.where(lane == 0, moved[1], moved[0])
    return jnp.concatenate([first, second], axis=0)


def time_vector(timestep, time_proj):
    half_freq = FREQ // 2
    steps_k = jnp.arange(half_freq, dtype=jnp.float32)
    frequency = jnp.exp(-jnp.log(10000.0) * steps_k / half_freq)
    angles = timestep[0].astype(jnp.float32) * frequency
    embedding = jnp.concatenate([jnp.cos(angles), jnp.sin(angles)])
    time_feature = jax.nn.silu(embedding).astype(jnp.bfloat16)
    return jnp.dot(time_feature[None, :], time_proj, preferred_element_type=jnp.float32).reshape(
        3, D
    )


def layer_norm(values):
    widened = values.astype(jnp.float32)
    average = jnp.mean(widened, axis=-1, keepdims=True)
    centred = widened - average
    variance = jnp.mean(centred * centred, axis=-1, keepdims=True)
    return centred * lax.rsqrt(variance + epsilon)


def attend(by_head, stale_full, patch):
    seq_rows = by_head.shape[0]
    image_rows = stale_full.shape[0]
    heads_here = by_head.shape[1] // (3 * HEAD_DIM)
    unpacked = by_head.reshape(seq_rows, heads_here, 3, HEAD_DIM)
    queries = unpacked[:, :, 0]
    fresh_kv = unpacked[:, :, 1:3].reshape(seq_rows, heads_here * 2 * HEAD_DIM)
    start_row = patch * seq_rows
    kv_all = lax.dynamic_update_slice(stale_full, fresh_kv, (start_row, jnp.zeros((), jnp.int32)))
    kv_heads = kv_all.reshape(image_rows, heads_here, 2, HEAD_DIM)
    keys_all = kv_heads[:, :, 0]
    values_all = kv_heads[:, :, 1]
    block_rows = math.gcd(seq_rows, 512)
    query_blocks = queries.reshape(seq_rows // block_rows, block_rows, heads_here, HEAD_DIM)
    inverse = HEAD_DIM ** (-0.5)

    def one_block(query_block):
        scores = (
            jnp.einsum("qhe,khe->hqk", query_block, keys_all, preferred_element_type=jnp.float32)
            * inverse
        )
        weights = jnp.exp(scores - jnp.max(scores, axis=2, keepdims=True))
        probability = (weights / jnp.sum(weights, axis=2, keepdims=True)).astype(jnp.bfloat16)
        return jnp.einsum(
            "hqk,khe->qhe", probability, values_all, preferred_element_type=jnp.float32
        ).astype(jnp.bfloat16)

    blocks_out = lax.map(one_block, query_blocks)
    return blocks_out.reshape(seq_rows, heads_here * HEAD_DIM)


def finish(finished, time_mod, final_table, final_weight):
    shift_row = final_table[0] + time_mod[0]
    scale_row = final_table[1] + time_mod[1]
    exit_normed = (layer_norm(finished) * (1.0 + scale_row) + shift_row).astype(jnp.bfloat16)
    return jnp.einsum(
        "fc,tf->ct", final_weight, exit_normed, preferred_element_type=jnp.float32
    ).astype(jnp.bfloat16)


def spread_exits(exits, segment_count):
    received = lax.all_to_all(exits, "segment", 0, 0, tiled=True)
    last = received[segment_count - 2 :]
    return jnp.transpose(last, (1, 0, 2))[..., None]


def body(
    arriving,
    entering,
    section_start,
    timestep,
    qkv_weight,
    out_weight,
    stale_kv,
    layer_table,
    time_proj,
    final_table,
    final_weight,
):
    segment_index = lax.axis_index("segment")
    segment_count = lax.axis_size("segment")
    groups = lax.axis_size("bx") * lax.axis_size("by")
    heads = groups * 2
    section = segment_index // 2
    lane = segment_index % 2
    sections = segment_count // 2
    time_mod = time_vector(timestep, time_proj)
    first_layer = jnp.sum(jnp.where(jnp.arange(sections) == section, section_start, 0))
    layer_rows = jnp.arange(layer_table.shape[0])[:, None, None] == first_layer
    table_row = jnp.sum(jnp.where(layer_rows, layer_table.astype(jnp.float32), 0.0), axis=0)
    modulation = table_row + time_mod
    own_parts = (qkv_weight[0], stale_kv[0])
    partner_parts = swapped(own_parts, "segment", 0)
    first_parts = [
        jnp.where(lane == 0, mine, other) for mine, other in zip(own_parts, partner_parts)
    ]
    second_parts = [
        jnp.where(lane == 0, other, mine) for mine, other in zip(own_parts, partner_parts)
    ]
    qkv_local = jnp.concatenate([first_parts[0], second_parts[0]], axis=0)
    stale_full = jnp.concatenate([first_parts[1], second_parts[1]], axis=0)
    out_head = head_rows(out_weight[0], heads)
    holding = arriving[0]
    exit_list = []
    for tick_index in range(TICKS):
        stream_id = jnp.where(
            section >= tick_index,
            2 * (section - tick_index) + lane,
            2 * (sections + tick_index - 1 - section) + lane,
        )
        patch = stream_id % PATCHES
        normed = (layer_norm(holding) * (1.0 + modulation[1]) + modulation[0]).astype(jnp.bfloat16)
        by_head = projected_tokens(normed, groups, qkv_local)
        head_out = attend(by_head, stale_full, patch)
        attended = scattered_sum(head_out, out_head, groups)
        finished = (holding.astype(jnp.float32) + modulation[2] * attended).astype(jnp.bfloat16)
        exit_list.append(finish(finished, time_mod, final_table, final_weight))
        passed = shifted(finished, "segment", 2)
        incoming = lax.dynamic_index_in_dim(entering[tick_index], lane, 0, keepdims=False)
        holding = jnp.where(segment_index < 2, incoming, passed)
    return (holding[None], spread_exits(jnp.stack(exit_list, axis=1), segment_count))


def solution(mesh):
    blk_size = mesh.shape["blk"]
    split = Mesh(
        mesh.devices.reshape(mesh.shape["segment"], blk_size // 4, 2, 2),
        ("segment",) + BLK,
    )
    in_specs = (
        P("segment", BLK, None),
        P(None, None, BLK, None),
        P(),
        P(),
        P("segment", None, BLK),
        P("segment", BLK, None),
        P("segment", None, BLK),
        P(),
        P(),
        P(),
        P(),
    )
    out_specs = (P("segment", BLK, None), P(None, None, BLK, "segment"))
    return jax.shard_map(body, mesh=split, in_specs=in_specs, out_specs=out_specs, check_vma=False)
```

```python
import math

import jax
import jax.numpy as jnp
from jax import lax
from jax.sharding import Mesh
from jax.sharding import PartitionSpec as P

D = 1152
FREQ = 256
TICKS = 2
PATCHES = 4
HEAD_DIM = 72

BLK = ("bx", "by", "bc")
SAME_CORE = ("bx", "by")
CORE = "bc"


epsilon = 1e-06


def swapped(value, axis, apart):
    mask = 2**apart
    pairs = [(source, source ^ mask) for source in range(lax.axis_size(axis))]
    return lax.ppermute(value, axis, pairs)


def core_swapped(value):
    return lax.ppermute(value, CORE, [(0, 1), (1, 0)])


def shifted(array, axis, by):
    peers = lax.axis_size(axis)
    pairs = [(i, i + by) for i in range(peers) if 0 <= i + by < peers]
    return lax.ppermute(array, axis, pairs)


def gathered_tokens(value, groups):
    copies = jnp.broadcast_to(value[None], (groups,) + value.shape)
    same_core = lax.all_to_all(copies, SAME_CORE, 0, 0, tiled=True)
    both = jnp.stack([same_core, core_swapped(same_core)])
    return both.reshape((2 * groups * value.shape[0],) + value.shape[1:])


def scattered_sum(head_out, out_head, groups):
    rows = head_out.shape[0] // 2
    theirs = jnp.dot(head_out[rows:], out_head, preferred_element_type=jnp.float32)
    moved = core_swapped(theirs.astype(jnp.bfloat16)).astype(jnp.float32)
    mine = lax.optimization_barrier(
        jnp.dot(head_out[:rows], out_head, preferred_element_type=jnp.float32)
    )
    summed = (mine + moved).astype(jnp.bfloat16).reshape(groups, -1, out_head.shape[1])
    received = lax.all_to_all(summed, SAME_CORE, 0, 0, tiled=True)
    return jnp.sum(received.astype(jnp.float32), axis=0)


def head_rows(out_rows, heads):
    segment_index = lax.axis_index("segment")
    lane = segment_index % 2
    per_half = heads // 2
    segments = lax.axis_size("segment")
    moved = []
    for flip in range(2):
        pairs = []
        for segment in range(segments):
            for j in range(heads):
                source_lane = segment % 2
                target_lane = (j % 2) ^ flip
                target = (segment - source_lane + target_lane) * heads + source_lane * per_half + j // 2
                pairs.append((segment * heads + j, target))
        moved.append(lax.ppermute(out_rows, ("segment",) + BLK, pairs))
    first = jnp.where(lane == 0, moved[0], moved[1])
    second = jnp.where(lane == 0, moved[1], moved[0])
    return jnp.concatenate([first, second], axis=0)


def time_vector(timestep, time_proj):
    half_freq = FREQ // 2
    steps_k = jnp.arange(half_freq, dtype=jnp.float32)
    frequency = jnp.exp(-jnp.log(10000.0) * steps_k / half_freq)
    angles = timestep[0].astype(jnp.float32) * frequency
    embedding = jnp.concatenate([jnp.cos(angles), jnp.sin(angles)])
    time_feature = jax.nn.silu(embedding).astype(jnp.bfloat16)
    return jnp.dot(time_feature[None, :], time_proj, preferred_element_type=jnp.float32).reshape(
        3, D
    )


def layer_norm(values):
    widened = values.astype(jnp.float32)
    average = jnp.mean(widened, axis=-1, keepdims=True)
    centred = widened - average
    variance = jnp.mean(centred * centred, axis=-1, keepdims=True)
    return centred * lax.rsqrt(variance + epsilon)


def attend(by_head, stale_full, patch):
    seq_rows = by_head.shape[0]
    image_rows = stale_full.shape[0]
    heads_here = by_head.shape[1] // (3 * HEAD_DIM)
    unpacked = by_head.reshape(seq_rows, heads_here, 3, HEAD_DIM)
    queries = unpacked[:, :, 0]
    fresh_kv = unpacked[:, :, 1:3].reshape(seq_rows, heads_here * 2 * HEAD_DIM)
    start_row = patch * seq_rows
    kv_all = lax.dynamic_update_slice(stale_full, fresh_kv, (start_row, jnp.zeros((), jnp.int32)))
    kv_heads = kv_all.reshape(image_rows, heads_here, 2, HEAD_DIM)
    keys_all = kv_heads[:, :, 0]
    values_all = kv_heads[:, :, 1]
    block_rows = math.gcd(seq_rows, 512)
    query_blocks = queries.reshape(seq_rows // block_rows, block_rows, heads_here, HEAD_DIM)
    inverse = HEAD_DIM ** (-0.5)

    def one_block(query_block):
        scores = (
            jnp.einsum("qhe,khe->hqk", query_block, keys_all, preferred_element_type=jnp.float32)
            * inverse
        )
        weights = jnp.exp(scores - jnp.max(scores, axis=2, keepdims=True))
        probability = (weights / jnp.sum(weights, axis=2, keepdims=True)).astype(jnp.bfloat16)
        return jnp.einsum(
            "hqk,khe->qhe", probability, values_all, preferred_element_type=jnp.float32
        ).astype(jnp.bfloat16)

    blocks_out = lax.map(one_block, query_blocks)
    return blocks_out.reshape(seq_rows, heads_here * HEAD_DIM)


def finish(finished, time_mod, final_table, final_weight):
    shift_row = final_table[0] + time_mod[0]
    scale_row = final_table[1] + time_mod[1]
    exit_normed = (layer_norm(finished) * (1.0 + scale_row) + shift_row).astype(jnp.bfloat16)
    return jnp.einsum(
        "fc,tf->ct", final_weight, exit_normed, preferred_element_type=jnp.float32
    ).astype(jnp.bfloat16)


def spread_exits(exits, segment_count):
    received = lax.all_to_all(exits, "segment", 0, 0, tiled=True)
    last = received[segment_count - 2 :]
    return jnp.transpose(last, (1, 0, 2))[..., None]


def body(
    arriving,
    entering,
    section_start,
    timestep,
    qkv_weight,
    out_weight,
    stale_kv,
    layer_table,
    time_proj,
    final_table,
    final_weight,
):
    segment_index = lax.axis_index("segment")
    segment_count = lax.axis_size("segment")
    groups = lax.axis_size("bx") * lax.axis_size("by")
    heads = groups * 2
    section = segment_index // 2
    lane = segment_index % 2
    sections = segment_count // 2
    time_mod = time_vector(timestep, time_proj)
    first_layer = jnp.sum(jnp.where(jnp.arange(sections) == section, section_start, 0))
    layer_rows = jnp.arange(layer_table.shape[0])[:, None, None] == first_layer
    table_row = jnp.sum(jnp.where(layer_rows, layer_table.astype(jnp.float32), 0.0), axis=0)
    modulation = table_row + time_mod
    own_parts = (qkv_weight[0], stale_kv[0])
    partner_parts = swapped(own_parts, "segment", 0)
    first_parts = [
        jnp.where(lane == 0, mine, other) for mine, other in zip(own_parts, partner_parts)
    ]
    second_parts = [
        jnp.where(lane == 0, other, mine) for mine, other in zip(own_parts, partner_parts)
    ]
    qkv_local = jnp.concatenate([first_parts[0], second_parts[0]], axis=0)
    stale_full = jnp.concatenate([first_parts[1], second_parts[1]], axis=0)
    holding = arriving[0]
    exit_list = []
    for tick_index in range(TICKS):
        stream_id = jnp.where(
            section >= tick_index,
            2 * (section - tick_index) + lane,
            2 * (sections + tick_index - 1 - section) + lane,
        )
        patch = stream_id % PATCHES
        normed = (layer_norm(holding) * (1.0 + modulation[1]) + modulation[0]).astype(jnp.bfloat16)
        tokens = gathered_tokens(normed, groups)
        if tick_index == 0:
            out_rows, tokens = lax.optimization_barrier((out_weight[0], tokens))
            out_head = head_rows(out_rows, heads)
        by_head = jnp.dot(tokens, qkv_local, preferred_element_type=jnp.float32).astype(jnp.bfloat16)
        head_out = attend(by_head, stale_full, patch)
        attended = scattered_sum(head_out, out_head, groups)
        finished = (holding.astype(jnp.float32) + modulation[2] * attended).astype(jnp.bfloat16)
        exit_list.append(finish(finished, time_mod, final_table, final_weight))
        passed = shifted(finished, "segment", 2)
        incoming = lax.dynamic_index_in_dim(entering[tick_index], lane, 0, keepdims=False)
        holding = jnp.where(segment_index < 2, incoming, passed)
    return (holding[None], spread_exits(jnp.stack(exit_list, axis=1), segment_count))


def solution(mesh):
    blk_size = mesh.shape["blk"]
    split = Mesh(
        mesh.devices.reshape(mesh.shape["segment"], blk_size // 4, 2, 2),
        ("segment",) + BLK,
    )
    in_specs = (
        P("segment", BLK, None),
        P(None, None, BLK, None),
        P(),
        P(),
        P("segment", None, BLK),
        P("segment", BLK, None),
        P("segment", None, BLK),
        P(),
        P(),
        P(),
        P(),
    )
    out_specs = (P("segment", BLK, None), P(None, None, BLK, "segment"))
    return jax.shard_map(body, mesh=split, in_specs=in_specs, out_specs=out_specs, check_vma=False)
```

```python
import math

import jax
import jax.numpy as jnp
from jax import lax
from jax.sharding import Mesh
from jax.sharding import PartitionSpec as P

D = 1152
FREQ = 256
TICKS = 2
PATCHES = 4
HEAD_DIM = 72

BLK = ("bx", "by", "bc")
SAME_CORE = ("bx", "by")
CORE = "bc"
SEG = ("sz", "sy")


epsilon = 1e-06


def swapped(value, peers, apart):
    mask = 2**apart
    pairs = [(source, source ^ mask) for source in range(peers)]
    return lax.ppermute(value, SEG, pairs)


def core_swapped(value):
    return lax.ppermute(value, CORE, [(0, 1), (1, 0)])


def shifted(array, peers, by):
    pairs = [(i, i + by) for i in range(peers) if 0 <= i + by < peers]
    return lax.ppermute(array, SEG, pairs)


def gathered_tokens(value, groups):
    copies = jnp.broadcast_to(value[None], (groups,) + value.shape)
    same_core = lax.all_to_all(copies, SAME_CORE, 0, 0, tiled=True)
    both = jnp.stack([same_core, core_swapped(same_core)])
    return both.reshape((2 * groups * value.shape[0],) + value.shape[1:])


def scattered_sum(head_out, out_head, groups):
    rows = head_out.shape[0] // 2
    theirs = jnp.dot(head_out[rows:], out_head, preferred_element_type=jnp.float32)
    moved = core_swapped(theirs.astype(jnp.bfloat16)).astype(jnp.float32)
    mine = lax.optimization_barrier(
        jnp.dot(head_out[:rows], out_head, preferred_element_type=jnp.float32)
    )
    summed = (mine + moved).astype(jnp.bfloat16).reshape(groups, -1, out_head.shape[1])
    received = lax.all_to_all(summed, SAME_CORE, 0, 0, tiled=True)
    return jnp.sum(received.astype(jnp.float32), axis=0)


def head_rows(out_rows, heads):
    segment_index = lax.axis_index(SEG)
    lane = segment_index % 2
    per_half = heads // 2
    segments = lax.axis_size("sz") * lax.axis_size("sy")
    moved = []
    for flip in range(2):
        pairs = []
        for segment in range(segments):
            for j in range(heads):
                source_lane = segment % 2
                target_lane = (j % 2) ^ flip
                target = (segment - source_lane + target_lane) * heads + source_lane * per_half + j // 2
                pairs.append((segment * heads + j, target))
        moved.append(lax.ppermute(out_rows, SEG + BLK, pairs))
    first = jnp.where(lane == 0, moved[0], moved[1])
    second = jnp.where(lane == 0, moved[1], moved[0])
    return jnp.concatenate([first, second], axis=0)


def time_vector(timestep, time_proj):
    half_freq = FREQ // 2
    steps_k = jnp.arange(half_freq, dtype=jnp.float32)
    frequency = jnp.exp(-jnp.log(10000.0) * steps_k / half_freq)
    angles = timestep[0].astype(jnp.float32) * frequency
    embedding = jnp.concatenate([jnp.cos(angles), jnp.sin(angles)])
    time_feature = jax.nn.silu(embedding).astype(jnp.bfloat16)
    return jnp.dot(time_feature[None, :], time_proj, preferred_element_type=jnp.float32).reshape(
        3, D
    )


def layer_norm(values):
    widened = values.astype(jnp.float32)
    average = jnp.mean(widened, axis=-1, keepdims=True)
    centred = widened - average
    variance = jnp.mean(centred * centred, axis=-1, keepdims=True)
    return centred * lax.rsqrt(variance + epsilon)


def attend(by_head, stale_full, patch):
    seq_rows = by_head.shape[0]
    image_rows = stale_full.shape[0]
    heads_here = by_head.shape[1] // (3 * HEAD_DIM)
    unpacked = by_head.reshape(seq_rows, heads_here, 3, HEAD_DIM)
    queries = unpacked[:, :, 0]
    fresh_kv = unpacked[:, :, 1:3].reshape(seq_rows, heads_here * 2 * HEAD_DIM)
    start_row = patch * seq_rows
    kv_all = lax.dynamic_update_slice(stale_full, fresh_kv, (start_row, jnp.zeros((), jnp.int32)))
    kv_heads = kv_all.reshape(image_rows, heads_here, 2, HEAD_DIM)
    keys_all = kv_heads[:, :, 0]
    values_all = kv_heads[:, :, 1]
    block_rows = math.gcd(seq_rows, 512)
    query_blocks = queries.reshape(seq_rows // block_rows, block_rows, heads_here, HEAD_DIM)
    inverse = HEAD_DIM ** (-0.5)

    def one_block(query_block):
        scores = (
            jnp.einsum("qhe,khe->hqk", query_block, keys_all, preferred_element_type=jnp.float32)
            * inverse
        )
        weights = jnp.exp(scores - jnp.max(scores, axis=2, keepdims=True))
        probability = (weights / jnp.sum(weights, axis=2, keepdims=True)).astype(jnp.bfloat16)
        return jnp.einsum(
            "hqk,khe->qhe", probability, values_all, preferred_element_type=jnp.float32
        ).astype(jnp.bfloat16)

    blocks_out = lax.map(one_block, query_blocks)
    return blocks_out.reshape(seq_rows, heads_here * HEAD_DIM)


def finish(finished, time_mod, final_table, final_weight):
    shift_row = final_table[0] + time_mod[0]
    scale_row = final_table[1] + time_mod[1]
    exit_normed = (layer_norm(finished) * (1.0 + scale_row) + shift_row).astype(jnp.bfloat16)
    return jnp.einsum(
        "fc,tf->ct", final_weight, exit_normed, preferred_element_type=jnp.float32
    ).astype(jnp.bfloat16)


def spread_exits(exits, rows, sources):
    by_row = exits.reshape((-1, rows) + exits.shape[1:]).swapaxes(0, 1)
    first = lax.all_to_all(by_row, "sy", 0, 0, tiled=True)
    from_sources = first[sources % rows :]
    by_plane = from_sources.swapaxes(0, 1)
    second = lax.all_to_all(by_plane, "sz", 0, 0, tiled=True)
    last = second[sources // rows]
    return jnp.transpose(last, (1, 0, 2))[..., None]


def body(
    arriving,
    entering,
    section_start,
    timestep,
    qkv_weight,
    out_weight,
    stale_kv,
    layer_table,
    time_proj,
    final_table,
    final_weight,
):
    segment_index = lax.axis_index(SEG)
    rows = lax.axis_size("sy")
    segment_count = lax.axis_size("sz") * rows
    groups = lax.axis_size("bx") * lax.axis_size("by")
    heads = groups * 2
    section = segment_index // 2
    lane = segment_index % 2
    sections = segment_count // 2
    time_mod = time_vector(timestep, time_proj)
    first_layer = jnp.sum(jnp.where(jnp.arange(sections) == section, section_start, 0))
    layer_rows = jnp.arange(layer_table.shape[0])[:, None, None] == first_layer
    table_row = jnp.sum(jnp.where(layer_rows, layer_table.astype(jnp.float32), 0.0), axis=0)
    modulation = table_row + time_mod
    own_parts = (qkv_weight[0], stale_kv[0])
    partner_parts = swapped(own_parts, segment_count, 0)
    first_parts = [
        jnp.where(lane == 0, mine, other) for mine, other in zip(own_parts, partner_parts)
    ]
    second_parts = [
        jnp.where(lane == 0, other, mine) for mine, other in zip(own_parts, partner_parts)
    ]
    qkv_local = jnp.concatenate([first_parts[0], second_parts[0]], axis=0)
    stale_full = jnp.concatenate([first_parts[1], second_parts[1]], axis=0)
    out_head = head_rows(out_weight[0], heads)
    holding = arriving[0]
    exit_list = []
    for tick_index in range(TICKS):
        stream_id = jnp.where(
            section >= tick_index,
            2 * (section - tick_index) + lane,
            2 * (sections + tick_index - 1 - section) + lane,
        )
        patch = stream_id % PATCHES
        normed = (layer_norm(holding) * (1.0 + modulation[1]) + modulation[0]).astype(jnp.bfloat16)
        by_head = jnp.dot(
            gathered_tokens(normed, groups),
            qkv_local,
            preferred_element_type=jnp.float32,
        ).astype(jnp.bfloat16)
        head_out = attend(by_head, stale_full, patch)
        attended = scattered_sum(head_out, out_head, groups)
        finished = (holding.astype(jnp.float32) + modulation[2] * attended).astype(jnp.bfloat16)
        exit_list.append(finish(finished, time_mod, final_table, final_weight))
        passed = shifted(finished, segment_count, 2)
        incoming = lax.dynamic_index_in_dim(entering[tick_index], lane, 0, keepdims=False)
        holding = jnp.where(segment_index < 2, incoming, passed)
    return (holding[None], spread_exits(jnp.stack(exit_list, axis=1), rows, segment_count - 2))


def solution(mesh):
    blk_size = mesh.shape["blk"]
    split = Mesh(
        mesh.devices.reshape(mesh.shape["segment"] // 4, 4, blk_size // 4, 2, 2),
        SEG + BLK,
    )
    in_specs = (
        P(SEG, BLK, None),
        P(None, None, BLK, None),
        P(),
        P(),
        P(SEG, None, BLK),
        P(SEG, BLK, None),
        P(SEG, None, BLK),
        P(),
        P(),
        P(),
        P(),
    )
    out_specs = (P(SEG, BLK, None), P(None, None, BLK, SEG))
    return jax.shard_map(body, mesh=split, in_specs=in_specs, out_specs=out_specs, check_vma=False)
```

```python
import math

import jax
import jax.numpy as jnp
from jax import lax
from jax.sharding import Mesh
from jax.sharding import PartitionSpec as P

D = 1152
FREQ = 256
TICKS = 2
PATCHES = 4
HEAD_DIM = 72

BLK = ("bx", "by", "bc")
SAME_CORE = ("bx", "by")
CORE = "bc"


epsilon = 1e-06


def swapped(value, axis, apart):
    mask = 2**apart
    pairs = [(source, source ^ mask) for source in range(lax.axis_size(axis))]
    return lax.ppermute(value, axis, pairs)


def core_swapped(value):
    return lax.ppermute(value, CORE, [(0, 1), (1, 0)])


def shifted(array, axis, by):
    peers = lax.axis_size(axis)
    pairs = [(i, i + by) for i in range(peers) if 0 <= i + by < peers]
    return lax.ppermute(array, axis, pairs)


def gathered_tokens(value, groups):
    copies = jnp.broadcast_to(value[None], (groups,) + value.shape)
    same_core = lax.all_to_all(copies, SAME_CORE, 0, 0, tiled=True)
    both = jnp.stack([same_core, core_swapped(same_core)])
    return both.reshape((2 * groups * value.shape[0],) + value.shape[1:])


def scattered_sum(head_out, out_head, groups):
    rows = head_out.shape[0] // 2
    theirs = jnp.dot(head_out[rows:], out_head, preferred_element_type=jnp.float32)
    moved = core_swapped(theirs.astype(jnp.bfloat16)).astype(jnp.float32)
    mine = lax.optimization_barrier(
        jnp.dot(head_out[:rows], out_head, preferred_element_type=jnp.float32)
    )
    summed = (mine + moved).astype(jnp.bfloat16).reshape(groups, -1, out_head.shape[1])
    received = lax.all_to_all(summed, SAME_CORE, 0, 0, tiled=True)
    return jnp.sum(received.astype(jnp.float32), axis=0)


def head_rows(out_rows, heads):
    segment_index = lax.axis_index("segment")
    lane = segment_index % 2
    per_half = heads // 2
    segments = lax.axis_size("segment")
    moved = []
    for flip in range(2):
        pairs = []
        for segment in range(segments):
            for j in range(heads):
                source_lane = segment % 2
                target_lane = (j % 2) ^ flip
                target = (segment - source_lane + target_lane) * heads + source_lane * per_half + j // 2
                pairs.append((segment * heads + j, target))
        moved.append(lax.ppermute(out_rows, ("segment",) + BLK, pairs))
    first = jnp.where(lane == 0, moved[0], moved[1])
    second = jnp.where(lane == 0, moved[1], moved[0])
    return jnp.concatenate([first, second], axis=0)


def time_vector(timestep, time_proj):
    half_freq = FREQ // 2
    steps_k = jnp.arange(half_freq, dtype=jnp.float32)
    frequency = jnp.exp(-jnp.log(10000.0) * steps_k / half_freq)
    angles = timestep[0].astype(jnp.float32) * frequency
    embedding = jnp.concatenate([jnp.cos(angles), jnp.sin(angles)])
    time_feature = jax.nn.silu(embedding).astype(jnp.bfloat16)
    return jnp.dot(time_feature[None, :], time_proj, preferred_element_type=jnp.float32).reshape(
        3, D
    )


def layer_norm(values):
    widened = values.astype(jnp.float32)
    average = jnp.mean(widened, axis=-1, keepdims=True)
    centred = widened - average
    variance = jnp.mean(centred * centred, axis=-1, keepdims=True)
    return centred * lax.rsqrt(variance + epsilon)


def attend(by_head, stale_full, patch):
    seq_rows = by_head.shape[0]
    image_rows = stale_full.shape[0]
    heads_here = by_head.shape[1] // (3 * HEAD_DIM)
    unpacked = by_head.reshape(seq_rows, heads_here, 3, HEAD_DIM)
    queries = unpacked[:, :, 0]
    fresh_kv = unpacked[:, :, 1:3].reshape(seq_rows, heads_here * 2 * HEAD_DIM)
    start_row = patch * seq_rows
    kv_all = lax.dynamic_update_slice(stale_full, fresh_kv, (start_row, jnp.zeros((), jnp.int32)))
    kv_heads = kv_all.reshape(image_rows, heads_here, 2, HEAD_DIM)
    keys_all = kv_heads[:, :, 0]
    values_all = kv_heads[:, :, 1]
    block_rows = math.gcd(seq_rows, 512)
    query_blocks = queries.reshape(seq_rows // block_rows, block_rows, heads_here, HEAD_DIM)
    inverse = HEAD_DIM ** (-0.5)

    def one_block(query_block):
        scores = (
            jnp.einsum("qhe,khe->hqk", query_block, keys_all, preferred_element_type=jnp.float32)
            * inverse
        )
        weights = jnp.exp(scores - jnp.max(scores, axis=2, keepdims=True))
        probability = (weights / jnp.sum(weights, axis=2, keepdims=True)).astype(jnp.bfloat16)
        return jnp.einsum(
            "hqk,khe->qhe", probability, values_all, preferred_element_type=jnp.float32
        ).astype(jnp.bfloat16)

    blocks_out = lax.map(one_block, query_blocks)
    return blocks_out.reshape(seq_rows, heads_here * HEAD_DIM)


def finish(finished, time_mod, final_table, final_weight):
    shift_row = final_table[0] + time_mod[0]
    scale_row = final_table[1] + time_mod[1]
    exit_normed = (layer_norm(finished) * (1.0 + scale_row) + shift_row).astype(jnp.bfloat16)
    return jnp.einsum(
        "fc,tf->ct", final_weight, exit_normed, preferred_element_type=jnp.float32
    ).astype(jnp.bfloat16)


def spread_exits(exits, segment_count):
    received = lax.all_to_all(exits, "segment", 0, 0, tiled=True)
    last = received[segment_count - 2 :]
    return jnp.transpose(last, (1, 0, 2))[..., None]


def body(
    arriving,
    entering,
    section_start,
    timestep,
    qkv_weight,
    out_weight,
    stale_kv,
    layer_table,
    time_proj,
    final_table,
    final_weight,
):
    segment_index = lax.axis_index("segment")
    segment_count = lax.axis_size("segment")
    groups = lax.axis_size("bx") * lax.axis_size("by")
    heads = groups * 2
    section = segment_index // 2
    lane = segment_index % 2
    sections = segment_count // 2
    time_mod = time_vector(timestep, time_proj)
    first_layer = jnp.sum(jnp.where(jnp.arange(sections) == section, section_start, 0))
    layer_rows = jnp.arange(layer_table.shape[0])[:, None, None] == first_layer
    table_row = jnp.sum(jnp.where(layer_rows, layer_table.astype(jnp.float32), 0.0), axis=0)
    modulation = table_row + time_mod
    own_qkv, own_stale = qkv_weight[0], stale_kv[0]
    partner_qkv, partner_stale = swapped((own_qkv, own_stale), "segment", 0)
    qkv_first = jnp.where(lane == 0, own_qkv, partner_qkv)
    qkv_second = jnp.where(lane == 0, partner_qkv, own_qkv)
    qkv_local = jnp.concatenate([qkv_first, qkv_second], axis=0)
    stale_full = jnp.concatenate([own_stale, partner_stale], axis=0)
    half_rows = own_stale.shape[0]
    out_head = head_rows(out_weight[0], heads)
    holding = arriving[0]
    exit_list = []
    for tick_index in range(TICKS):
        stream_id = jnp.where(
            section >= tick_index,
            2 * (section - tick_index) + lane,
            2 * (sections + tick_index - 1 - section) + lane,
        )
        patch = stream_id % PATCHES
        normed = (layer_norm(holding) * (1.0 + modulation[1]) + modulation[0]).astype(jnp.bfloat16)
        by_head = jnp.dot(
            gathered_tokens(normed, groups),
            qkv_local,
            preferred_element_type=jnp.float32,
        ).astype(jnp.bfloat16)
        patches_per_half = half_rows // by_head.shape[0]
        local_patch = jnp.where(patch // patches_per_half == lane, 0, patches_per_half) + (
            patch % patches_per_half
        )
        head_out = attend(by_head, stale_full, local_patch)
        attended = scattered_sum(head_out, out_head, groups)
        finished = (holding.astype(jnp.float32) + modulation[2] * attended).astype(jnp.bfloat16)
        exit_list.append(finish(finished, time_mod, final_table, final_weight))
        passed = shifted(finished, "segment", 2)
        incoming = lax.dynamic_index_in_dim(entering[tick_index], lane, 0, keepdims=False)
        holding = jnp.where(segment_index < 2, incoming, passed)
    return (holding[None], spread_exits(jnp.stack(exit_list, axis=1), segment_count))


def solution(mesh):
    blk_size = mesh.shape["blk"]
    split = Mesh(
        mesh.devices.reshape(mesh.shape["segment"], blk_size // 4, 2, 2),
        ("segment",) + BLK,
    )
    in_specs = (
        P("segment", BLK, None),
        P(None, None, BLK, None),
        P(),
        P(),
        P("segment", None, BLK),
        P("segment", BLK, None),
        P("segment", None, BLK),
        P(),
        P(),
        P(),
        P(),
    )
    out_specs = (P("segment", BLK, None), P(None, None, BLK, "segment"))
    return jax.shard_map(body, mesh=split, in_specs=in_specs, out_specs=out_specs, check_vma=False)
```

```python
import math

import jax
import jax.numpy as jnp
from jax import lax
from jax.sharding import Mesh
from jax.sharding import PartitionSpec as P

D = 1152
FREQ = 256
TICKS = 2
PATCHES = 4
HEAD_DIM = 72

BLK = ("bx", "by", "bc")
SAME_CORE = ("bx", "by")
CORE = "bc"


epsilon = 1e-06


def swapped(value, axis, apart):
    mask = 2**apart
    pairs = [(source, source ^ mask) for source in range(lax.axis_size(axis))]
    return lax.ppermute(value, axis, pairs)


def core_swapped(value):
    return lax.ppermute(value, CORE, [(0, 1), (1, 0)])


def shifted(array, axis, by):
    peers = lax.axis_size(axis)
    pairs = [(i, i + by) for i in range(peers) if 0 <= i + by < peers]
    return lax.ppermute(array, axis, pairs)


def gathered_tokens(value, groups):
    copies = jnp.broadcast_to(value[None], (groups,) + value.shape)
    same_core = lax.all_to_all(copies, SAME_CORE, 0, 0, tiled=True)
    both = jnp.stack([same_core, core_swapped(same_core)])
    return both.reshape((2 * groups * value.shape[0],) + value.shape[1:])


def scattered_sum(head_out, out_head, groups):
    rows = head_out.shape[0] // 2
    theirs = jnp.dot(head_out[rows:], out_head, preferred_element_type=jnp.float32)
    moved = core_swapped(theirs.astype(jnp.bfloat16)).astype(jnp.float32)
    mine = lax.optimization_barrier(
        jnp.dot(head_out[:rows], out_head, preferred_element_type=jnp.float32)
    )
    summed = (mine + moved).astype(jnp.bfloat16).reshape(groups, -1, out_head.shape[1])
    received = lax.all_to_all(summed, SAME_CORE, 0, 0, tiled=True)
    return jnp.sum(received.astype(jnp.float32), axis=0)


def head_rows(out_rows, heads):
    segment_index = lax.axis_index("segment")
    lane = segment_index % 2
    per_half = heads // 2
    segments = lax.axis_size("segment")
    moved = []
    for flip in range(2):
        pairs = []
        for segment in range(segments):
            for j in range(heads):
                source_lane = segment % 2
                target_lane = (j % 2) ^ flip
                target = (segment - source_lane + target_lane) * heads + source_lane * per_half + j // 2
                pairs.append((segment * heads + j, target))
        moved.append(lax.ppermute(out_rows, ("segment",) + BLK, pairs))
    first = jnp.where(lane == 0, moved[0], moved[1])
    second = jnp.where(lane == 0, moved[1], moved[0])
    return jnp.concatenate([first, second], axis=0)


def time_vector(timestep, time_proj):
    half_freq = FREQ // 2
    steps_k = jnp.arange(half_freq, dtype=jnp.float32)
    frequency = jnp.exp(-jnp.log(10000.0) * steps_k / half_freq)
    angles = timestep[0].astype(jnp.float32) * frequency
    embedding = jnp.concatenate([jnp.cos(angles), jnp.sin(angles)])
    time_feature = jax.nn.silu(embedding).astype(jnp.bfloat16)
    return jnp.dot(time_feature[None, :], time_proj, preferred_element_type=jnp.float32).reshape(
        3, D
    )


def layer_norm(values):
    widened = values.astype(jnp.float32)
    average = jnp.mean(widened, axis=-1, keepdims=True)
    centred = widened - average
    variance = jnp.mean(centred * centred, axis=-1, keepdims=True)
    return centred * lax.rsqrt(variance + epsilon)


def attend(by_head, stale_full, patch):
    seq_rows = by_head.shape[0]
    image_rows = stale_full.shape[0]
    heads_here = by_head.shape[1] // (3 * HEAD_DIM)
    unpacked = by_head.reshape(seq_rows, heads_here, 3, HEAD_DIM)
    queries = unpacked[:, :, 0]
    fresh_kv = unpacked[:, :, 1:3].reshape(seq_rows, heads_here * 2 * HEAD_DIM)
    start_row = patch * seq_rows
    kv_all = lax.dynamic_update_slice(stale_full, fresh_kv, (start_row, jnp.zeros((), jnp.int32)))
    kv_heads = kv_all.reshape(image_rows, heads_here, 2, HEAD_DIM)
    keys_all = kv_heads[:, :, 0]
    values_all = kv_heads[:, :, 1]
    block_rows = math.gcd(seq_rows, 512)
    query_blocks = queries.reshape(seq_rows // block_rows, block_rows, heads_here, HEAD_DIM)
    inverse = HEAD_DIM ** (-0.5)

    def one_block(query_block):
        scores = (
            jnp.einsum("qhe,khe->hqk", query_block, keys_all, preferred_element_type=jnp.float32)
            * inverse
        )
        weights = jnp.exp(scores - jnp.max(scores, axis=2, keepdims=True))
        probability = (weights / jnp.sum(weights, axis=2, keepdims=True)).astype(jnp.bfloat16)
        return jnp.einsum(
            "hqk,khe->qhe", probability, values_all, preferred_element_type=jnp.float32
        ).astype(jnp.bfloat16)

    blocks_out = lax.map(one_block, query_blocks)
    return blocks_out.reshape(seq_rows, heads_here * HEAD_DIM)


def finish(finished, time_mod, final_table, final_weight):
    shift_row = final_table[0] + time_mod[0]
    scale_row = final_table[1] + time_mod[1]
    exit_normed = (layer_norm(finished) * (1.0 + scale_row) + shift_row).astype(jnp.bfloat16)
    return jnp.einsum(
        "fc,tf->ct", final_weight, exit_normed, preferred_element_type=jnp.float32
    ).astype(jnp.bfloat16)


def spread_exits(exits, segment_count):
    received = lax.all_to_all(exits, "segment", 0, 0, tiled=True)
    last = received[segment_count - 2 :]
    return jnp.transpose(last, (1, 0, 2))[..., None]


def body(
    arriving,
    entering,
    section_start,
    timestep,
    qkv_weight,
    out_weight,
    stale_kv,
    layer_table,
    time_proj,
    final_table,
    final_weight,
):
    segment_index = lax.axis_index("segment")
    segment_count = lax.axis_size("segment")
    groups = lax.axis_size("bx") * lax.axis_size("by")
    heads = groups * 2
    section = segment_index // 2
    lane = segment_index % 2
    sections = segment_count // 2
    time_mod = time_vector(timestep, time_proj)
    first_layer = jnp.sum(jnp.where(jnp.arange(sections) == section, section_start, 0))
    layer_rows = jnp.arange(layer_table.shape[0])[:, None, None] == first_layer
    table_row = jnp.sum(jnp.where(layer_rows, layer_table.astype(jnp.float32), 0.0), axis=0)
    modulation = table_row + time_mod
    own_qkv, own_stale = qkv_weight[0], stale_kv[0]
    partner_qkv, partner_stale = swapped((own_qkv, own_stale), "segment", 0)
    half_inputs = own_qkv.shape[0]
    zero = jnp.zeros((), jnp.int32)
    placed = lax.dynamic_update_slice(
        jnp.concatenate([own_qkv, own_qkv], axis=0), own_qkv, (lane * half_inputs, zero)
    )
    qkv_local = lax.dynamic_update_slice(placed, partner_qkv, ((1 - lane) * half_inputs, zero))
    stale_full = jnp.concatenate([own_stale, partner_stale], axis=0)
    half_rows = own_stale.shape[0]
    out_head = head_rows(out_weight[0], heads)
    holding = arriving[0]
    exit_list = []
    for tick_index in range(TICKS):
        stream_id = jnp.where(
            section >= tick_index,
            2 * (section - tick_index) + lane,
            2 * (sections + tick_index - 1 - section) + lane,
        )
        patch = stream_id % PATCHES
        normed = (layer_norm(holding) * (1.0 + modulation[1]) + modulation[0]).astype(jnp.bfloat16)
        by_head = jnp.dot(
            gathered_tokens(normed, groups),
            qkv_local,
            preferred_element_type=jnp.float32,
        ).astype(jnp.bfloat16)
        patches_per_half = half_rows // by_head.shape[0]
        local_patch = jnp.where(patch // patches_per_half == lane, 0, patches_per_half) + (
            patch % patches_per_half
        )
        head_out = attend(by_head, stale_full, local_patch)
        attended = scattered_sum(head_out, out_head, groups)
        finished = (holding.astype(jnp.float32) + modulation[2] * attended).astype(jnp.bfloat16)
        exit_list.append(finish(finished, time_mod, final_table, final_weight))
        passed = shifted(finished, "segment", 2)
        incoming = lax.dynamic_index_in_dim(entering[tick_index], lane, 0, keepdims=False)
        holding = jnp.where(segment_index < 2, incoming, passed)
    return (holding[None], spread_exits(jnp.stack(exit_list, axis=1), segment_count))


def solution(mesh):
    blk_size = mesh.shape["blk"]
    split = Mesh(
        mesh.devices.reshape(mesh.shape["segment"], blk_size // 4, 2, 2),
        ("segment",) + BLK,
    )
    in_specs = (
        P("segment", BLK, None),
        P(None, None, BLK, None),
        P(),
        P(),
        P("segment", None, BLK),
        P("segment", BLK, None),
        P("segment", None, BLK),
        P(),
        P(),
        P(),
        P(),
    )
    out_specs = (P("segment", BLK, None), P(None, None, BLK, "segment"))
    return jax.shard_map(body, mesh=split, in_specs=in_specs, out_specs=out_specs, check_vma=False)
```

```python
import math

import jax
import jax.numpy as jnp
from jax import lax
from jax.sharding import Mesh
from jax.sharding import PartitionSpec as P

D = 1152
FREQ = 256
TICKS = 2
PATCHES = 4
HEAD_DIM = 72

BLK = ("bx", "by", "bc")
SAME_CORE = ("bx", "by")
CORE = "bc"


epsilon = 1e-06


def swapped(value, axis, apart):
    mask = 2**apart
    pairs = [(source, source ^ mask) for source in range(lax.axis_size(axis))]
    return lax.ppermute(value, axis, pairs)


def core_swapped(value):
    return lax.ppermute(value, CORE, [(0, 1), (1, 0)])


def shifted(array, axis, by):
    peers = lax.axis_size(axis)
    pairs = [(i, i + by) for i in range(peers) if 0 <= i + by < peers]
    return lax.ppermute(array, axis, pairs)


def gathered_tokens(value, groups):
    copies = jnp.broadcast_to(value[None], (groups,) + value.shape)
    same_core = lax.all_to_all(copies, SAME_CORE, 0, 0, tiled=True)
    both = jnp.stack([same_core, core_swapped(same_core)])
    return both.reshape((2 * groups * value.shape[0],) + value.shape[1:])


def scattered_sum(head_out, out_head, groups):
    rows = head_out.shape[0] // 2
    theirs = jnp.dot(head_out[rows:], out_head, preferred_element_type=jnp.float32)
    moved = core_swapped(theirs.astype(jnp.bfloat16)).astype(jnp.float32)
    mine = lax.optimization_barrier(
        jnp.dot(head_out[:rows], out_head, preferred_element_type=jnp.float32)
    )
    summed = (mine + moved).astype(jnp.bfloat16).reshape(groups, -1, out_head.shape[1])
    received = lax.all_to_all(summed, SAME_CORE, 0, 0, tiled=True)
    return jnp.sum(received.astype(jnp.float32), axis=0)


def head_rows(out_rows, heads):
    segment_index = lax.axis_index("segment")
    lane = segment_index % 2
    per_half = heads // 2
    segments = lax.axis_size("segment")
    moved = []
    for flip in range(2):
        pairs = []
        for segment in range(segments):
            for j in range(heads):
                source_lane = segment % 2
                target_lane = (j % 2) ^ flip
                target = (segment - source_lane + target_lane) * heads + source_lane * per_half + j // 2
                pairs.append((segment * heads + j, target))
        moved.append(lax.ppermute(out_rows, ("segment",) + BLK, pairs))
    first = jnp.where(lane == 0, moved[0], moved[1])
    second = jnp.where(lane == 0, moved[1], moved[0])
    return jnp.concatenate([first, second], axis=0)


def time_vector(timestep, time_proj):
    half_freq = FREQ // 2
    steps_k = jnp.arange(half_freq, dtype=jnp.float32)
    frequency = jnp.exp(-jnp.log(10000.0) * steps_k / half_freq)
    angles = timestep[0].astype(jnp.float32) * frequency
    embedding = jnp.concatenate([jnp.cos(angles), jnp.sin(angles)])
    time_feature = jax.nn.silu(embedding).astype(jnp.bfloat16)
    return jnp.dot(time_feature[None, :], time_proj, preferred_element_type=jnp.float32).reshape(
        3, D
    )


def layer_norm(values):
    widened = values.astype(jnp.float32)
    average = jnp.mean(widened, axis=-1, keepdims=True)
    centred = widened - average
    variance = jnp.mean(centred * centred, axis=-1, keepdims=True)
    return centred * lax.rsqrt(variance + epsilon)


def attend(by_head, stale_full, patch):
    seq_rows = by_head.shape[0]
    image_rows = stale_full.shape[0]
    heads_here = by_head.shape[1] // (3 * HEAD_DIM)
    unpacked = by_head.reshape(seq_rows, heads_here, 3, HEAD_DIM)
    queries = unpacked[:, :, 0]
    fresh_kv = unpacked[:, :, 1:3].reshape(seq_rows, heads_here * 2 * HEAD_DIM)
    start_row = patch * seq_rows
    kv_all = lax.dynamic_update_slice(stale_full, fresh_kv, (start_row, jnp.zeros((), jnp.int32)))
    kv_heads = kv_all.reshape(image_rows, heads_here, 2, HEAD_DIM)
    keys_all = kv_heads[:, :, 0]
    values_all = kv_heads[:, :, 1]
    block_rows = math.gcd(seq_rows, 512)
    query_blocks = queries.reshape(seq_rows // block_rows, block_rows, heads_here, HEAD_DIM)
    inverse = HEAD_DIM ** (-0.5)

    def one_block(query_block):
        scores = (
            jnp.einsum("qhe,khe->hqk", query_block, keys_all, preferred_element_type=jnp.float32)
            * inverse
        )
        weights = jnp.exp(scores - jnp.max(scores, axis=2, keepdims=True))
        probability = (weights / jnp.sum(weights, axis=2, keepdims=True)).astype(jnp.bfloat16)
        return jnp.einsum(
            "hqk,khe->qhe", probability, values_all, preferred_element_type=jnp.float32
        ).astype(jnp.bfloat16)

    blocks_out = lax.map(one_block, query_blocks)
    return blocks_out.reshape(seq_rows, heads_here * HEAD_DIM)


def finish(finished, time_mod, final_table):
    shift_row = final_table[0] + time_mod[0]
    scale_row = final_table[1] + time_mod[1]
    return (layer_norm(finished) * (1.0 + scale_row) + shift_row).astype(jnp.bfloat16)


def spread_exits(exits, segment_count):
    received = lax.all_to_all(exits, "segment", 0, 0, tiled=True)
    last = received[segment_count - 2 :]
    return jnp.transpose(last, (1, 0, 2))[..., None]


def body(
    arriving,
    entering,
    section_start,
    timestep,
    qkv_weight,
    out_weight,
    stale_kv,
    layer_table,
    time_proj,
    final_table,
    final_weight,
):
    segment_index = lax.axis_index("segment")
    segment_count = lax.axis_size("segment")
    groups = lax.axis_size("bx") * lax.axis_size("by")
    heads = groups * 2
    section = segment_index // 2
    lane = segment_index % 2
    sections = segment_count // 2
    time_mod = time_vector(timestep, time_proj)
    first_layer = jnp.sum(jnp.where(jnp.arange(sections) == section, section_start, 0))
    layer_rows = jnp.arange(layer_table.shape[0])[:, None, None] == first_layer
    table_row = jnp.sum(jnp.where(layer_rows, layer_table.astype(jnp.float32), 0.0), axis=0)
    modulation = table_row + time_mod
    own_qkv, own_stale = qkv_weight[0], stale_kv[0]
    partner_qkv, partner_stale = swapped((own_qkv, own_stale), "segment", 0)
    qkv_first = jnp.where(lane == 0, own_qkv, partner_qkv)
    qkv_second = jnp.where(lane == 0, partner_qkv, own_qkv)
    qkv_local = jnp.concatenate([qkv_first, qkv_second], axis=0)
    stale_full = jnp.concatenate([own_stale, partner_stale], axis=0)
    half_rows = own_stale.shape[0]
    out_head = head_rows(out_weight[0], heads)
    holding = arriving[0]
    exit_list = []
    for tick_index in range(TICKS):
        stream_id = jnp.where(
            section >= tick_index,
            2 * (section - tick_index) + lane,
            2 * (sections + tick_index - 1 - section) + lane,
        )
        patch = stream_id % PATCHES
        normed = (layer_norm(holding) * (1.0 + modulation[1]) + modulation[0]).astype(jnp.bfloat16)
        by_head = jnp.dot(
            gathered_tokens(normed, groups),
            qkv_local,
            preferred_element_type=jnp.float32,
        ).astype(jnp.bfloat16)
        patches_per_half = half_rows // by_head.shape[0]
        local_patch = jnp.where(patch // patches_per_half == lane, 0, patches_per_half) + (
            patch % patches_per_half
        )
        head_out = attend(by_head, stale_full, local_patch)
        attended = scattered_sum(head_out, out_head, groups)
        finished = (holding.astype(jnp.float32) + modulation[2] * attended).astype(jnp.bfloat16)
        exit_list.append(finish(finished, time_mod, final_table))
        passed = shifted(finished, "segment", 2)
        incoming = lax.dynamic_index_in_dim(entering[tick_index], lane, 0, keepdims=False)
        holding = jnp.where(segment_index < 2, incoming, passed)
    return (holding[None], spread_exits(
            jnp.einsum(
                "fc,utf->cut", final_weight, jnp.stack(exit_list), preferred_element_type=jnp.float32
            ).astype(jnp.bfloat16),
            segment_count,
        ))


def solution(mesh):
    blk_size = mesh.shape["blk"]
    split = Mesh(
        mesh.devices.reshape(mesh.shape["segment"], blk_size // 4, 2, 2),
        ("segment",) + BLK,
    )
    in_specs = (
        P("segment", BLK, None),
        P(None, None, BLK, None),
        P(),
        P(),
        P("segment", None, BLK),
        P("segment", BLK, None),
        P("segment", None, BLK),
        P(),
        P(),
        P(),
        P(),
    )
    out_specs = (P("segment", BLK, None), P(None, None, BLK, "segment"))
    return jax.shard_map(body, mesh=split, in_specs=in_specs, out_specs=out_specs, check_vma=False)
```
